32 devices in a mesh: parts: 2 (over y), pix: 16 (over z, x, core).
Axes of the slice: x: 2, y: 2, z: 4, core: 2. Of those that a mesh axis runs over, the one named last changes fastest.
Arguments:
- clip_pixels: bfloat16 [256, 64, 1024], P('parts', 'pix'), parts along dimension 0, may hold values from -6 to 6
- cotangent: bfloat16 [256, 64, 4096], P('parts', 'pix'), parts along dimension 0, may hold values from -0.029907227 to 0.029907227
- master_weights: float32 [368640], P(('parts', 'pix')), parts along dimension 0, may hold values from -0.25 to 0.25
- first_moment: float32 [368640], P(('parts', 'pix')), parts along dimension 0, may hold values from -6 to 6
- second_moment: float32 [368640], P(('parts', 'pix')), parts along dimension 0, may hold values from 0.25 to 4
Outputs:
- adam_step: float32 [368640], P(('parts', 'pix')), parts along dimension 0
- new_weights: bfloat16 [368640], P('parts'), parts along dimension 0
The draws below stay inside these ranges and needn't reach their ends.
There are 2 independent parts, one for each index of `parts`. The reference program is written for one: setup_inputs(seed, part) draws one part's arguments, and reference() takes and returns one part's arrays. A program takes and returns all parts, laid end to end along the dimension named above; each array names one. Nothing has to cross between parts.
All inputs are finite; a program needn't handle non-finite values.
Results may differ from the reference program's by a relative error of at most 0.0017.
Values may be sent and summed in bfloat16 or wider, within the bound.
No kernel may reach another device: no remote copies, remote signals or barrier semaphores. Data moves between devices by JAX's collectives and lax.ppermute only.
A program may use at most 256 MiB of HBM per device.

```python
import math
import jax
import jax.numpy as jnp
from jax import lax

C = 64
COUT = 256
LAYERS = 3
CLEN = 32
CLIPS = 4
W = 16
FRAMES = 128
H = 64
NPAR = 184320


def block_levels(own_key, dims, cuts, low, largest):
    factor_of, own = 1.0, jax.random.fold_in(own_key, 6)
    for position, parts in cuts:
        heights = jnp.exp(jax.random.uniform(jax.random.fold_in(own, position), (parts,), jnp.float32, low / len(cuts), largest / len(cuts)))
        factor_of = factor_of * jnp.repeat(heights, dims[position] // parts).reshape([-1 if axis == position else 1 for axis in range(len(dims))])
    return factor_of


def scatter_about(key, extent, deviation, limit, shards=(), kind=jnp.bfloat16):
    gain = block_levels(key, extent, shards, -0.22, 0.18) if shards else 1.0
    result = jax.random.normal(key, extent, jnp.float32) * deviation * gain
    return jnp.minimum(jnp.maximum(result, -limit), limit).astype(kind)


def setup_inputs(seed: int = 0, part: int = 0) -> dict:
    splits = jax.random.split(jax.random.key(seed), 6)
    part_splits = jax.random.split(jax.random.fold_in(splits[5], part), 6)
    clip_pixels = scatter_about(part_splits[0], (FRAMES, H, W * C), 1.0, 6.0, ((1, 16),))
    cotangent = scatter_about(part_splits[1], (FRAMES, H, W * COUT), 0.005, 0.029907227, ((1, 16),))
    master_weights = scatter_about(part_splits[2], (NPAR,), (9 * C) ** -0.5, 0.25, ((0, 16),), jnp.float32)
    first_moment = scatter_about(part_splits[3], (NPAR,), 1.0, 6.0, ((0, 16),), jnp.float32)
    second_moment = jnp.clip(jnp.exp(math.log(4.0) - 2.7725887 * jax.random.uniform(part_splits[4], (NPAR,), jnp.float32) ** block_levels(part_splits[4], (NPAR,), ((0, 16),), -0.2, 0.2)), 0.25, 4.0)
    return {"clip_pixels": clip_pixels, "cotangent": cotangent, "master_weights": master_weights, "first_moment": first_moment, "second_moment": second_moment}


def silu_slope(value):
    sigma = jax.nn.sigmoid(value)
    return sigma * (1.0 + value * (1.0 - sigma))

def temporal_apply(hidden, weights, spread):
    length = hidden.shape[1]
    padded = jnp.pad(hidden, ((0, 0), (spread, spread), (0, 0), (0, 0))).astype(jnp.float32)
    summed = jnp.zeros(hidden.shape[:3] + (weights.shape[2],), jnp.float32)
    for kernel_tap in range(3):
        start = kernel_tap * spread
        summed = summed + jnp.einsum('clpi,io->clpo', padded[:, start:start + length], weights[kernel_tap].astype(jnp.float32))
    return summed

def temporal_transpose(slope_grad, weights, spread):
    length = slope_grad.shape[1]
    padded = jnp.pad(slope_grad, ((0, 0), (spread, spread), (0, 0), (0, 0))).astype(jnp.float32)
    summed = jnp.zeros(slope_grad.shape[:3] + (weights.shape[1],), jnp.float32)
    for kernel_tap in range(3):
        start = (2 - kernel_tap) * spread
        summed = summed + jnp.einsum('clpo,io->clpi', padded[:, start:start + length], weights[kernel_tap].astype(jnp.float32))
    return summed

def temporal_wgrad(hidden, slope_grad, spread):
    length = hidden.shape[1]
    padded = jnp.pad(hidden, ((0, 0), (spread, spread), (0, 0), (0, 0))).astype(jnp.float32)
    taps_out = []
    for kernel_tap in range(3):
        start = kernel_tap * spread
        taps_out.append(jnp.einsum('clpi,clpo->io', padded[:, start:start + length], slope_grad.astype(jnp.float32)))
    return jnp.stack(taps_out)

def frame_backward(frame_hidden, frame_cot, spatial_w):
    height, width = (frame_hidden.shape[0], frame_hidden.shape[1])
    padded = jnp.pad(frame_hidden, ((1, 1), (1, 1), (0, 0))).astype(jnp.float32)
    output = jnp.zeros((height, width, spatial_w.shape[2]), jnp.float32)
    for row_tap in range(3):
        for col_tap in range(3):
            output = output + jnp.einsum('hwi,io->hwo', padded[row_tap:row_tap + height, col_tap:col_tap + width], spatial_w[3 * row_tap + col_tap].astype(jnp.float32))
    slope_grad = (frame_cot.astype(jnp.float32) * silu_slope(output)).astype(jnp.bfloat16)
    grad_taps = []
    for row_tap in range(3):
        for col_tap in range(3):
            grad_taps.append(jnp.einsum('hwi,hwo->io', padded[row_tap:row_tap + height, col_tap:col_tap + width], slope_grad.astype(jnp.float32)))
    padded_grad = jnp.pad(slope_grad, ((1, 1), (1, 1), (0, 0))).astype(jnp.float32)
    back = jnp.zeros((height, width, spatial_w.shape[1]), jnp.float32)
    for row_tap in range(3):
        for col_tap in range(3):
            back = back + jnp.einsum('hwo,io->hwi', padded_grad[2 - row_tap:2 - row_tap + height, 2 - col_tap:2 - col_tap + width], spatial_w[3 * row_tap + col_tap].astype(jnp.float32))
    return (jnp.stack(grad_taps), back.astype(jnp.bfloat16))

def reference(clip_pixels, cotangent, master_weights, first_moment, second_moment):
    weights_bf = master_weights.astype(jnp.bfloat16)
    split_at = 9 * C * COUT
    spatial_w = weights_bf[:split_at].reshape(9, C, COUT)
    temporal_w = weights_bf[split_at:].reshape(LAYERS, 3, C, C)
    hidden = clip_pixels.reshape(CLIPS, CLEN, H * W, C)
    inputs = []
    preacts = []
    for layer_index in range(LAYERS):
        spread = 2 ** layer_index
        inputs.append(hidden)
        preact = temporal_apply(hidden, temporal_w[layer_index], spread)
        preacts.append(preact)
        hidden = (hidden.astype(jnp.float32) + jax.nn.silu(preact)).astype(jnp.bfloat16)
    frames_hidden = hidden.reshape(FRAMES, H, W, C)
    frames_cot = cotangent.reshape(FRAMES, H, W, COUT)

    def one_frame(carried, pair):
        grad_taps, back = frame_backward(pair[0], pair[1], spatial_w)
        return (carried + grad_taps, back)
    grad_spatial, dh_frames = lax.scan(one_frame, jnp.zeros((9, C, COUT), jnp.float32), (frames_hidden, frames_cot))
    carried_grad = dh_frames.reshape(CLIPS, CLEN, H * W, C).astype(jnp.float32)
    layer_grads = [None] * LAYERS
    for layer_index in reversed(range(LAYERS)):
        spread = 2 ** layer_index
        slope_grad = (carried_grad * silu_slope(preacts[layer_index])).astype(jnp.bfloat16)
        layer_grads[layer_index] = temporal_wgrad(inputs[layer_index], slope_grad, spread)
        if layer_index > 0:
            carried_grad = carried_grad + temporal_transpose(slope_grad, temporal_w[layer_index], spread)
    grad_all = jnp.concatenate([grad_spatial.reshape(-1), jnp.stack(layer_grads).reshape(-1)])
    moment_one = 0.9 * first_moment + 0.1 * grad_all
    moment_two = 0.95 * second_moment + 0.05 * grad_all * grad_all
    adam_step = moment_one / (jnp.sqrt(moment_two) + 1e-08)
    new_weights = (master_weights - 0.001 * adam_step).astype(jnp.bfloat16)
    return (adam_step, new_weights)
```

```python
import jax
import jax.numpy as jnp
from jax import lax
from jax.sharding import PartitionSpec as P

C = 64
COUT = 256
LAYERS = 3
CLEN = 32
W = 16


def extended_2(cells, sides, width):
    for axis, dim in sides:
        count = lax.axis_size(axis)
        ends = count - 1
        head = lax.slice_in_dim(cells, 0, width, axis=dim)
        tail = lax.slice_in_dim(cells, cells.shape[dim] - width, cells.shape[dim], axis=dim)
        cells = jnp.concatenate(
            [
                lax.ppermute(tail, axis, [(i, (i + 1) % count) for i in range(ends)]),
                cells,
                lax.ppermute(head, axis, [((i + 1) % count, i) for i in range(ends)]),
            ],
            axis=dim,
        )
    return cells


def tree_sum_scatter(values, axis):
    count = lax.axis_size(axis)
    me = lax.axis_index(axis)
    blocks = values.reshape(count, -1)
    step = 0
    while (1 << step) < count:
        bit = (me >> step) & 1
        blocks = blocks.reshape(blocks.shape[0] // 2, 2, blocks.shape[1])
        low, high = blocks[:, 0], blocks[:, 1]
        keep = jnp.where(bit == 1, high, low)
        send = jnp.where(bit == 1, low, high)
        blocks = keep + lax.ppermute(send, axis, [(j, j ^ (1 << step)) for j in range(count)])
        step += 1
    return blocks.reshape(-1)


def tree_gather(values, axis):
    count = lax.axis_size(axis)
    me = lax.axis_index(axis)
    blocks = values.reshape(1, -1)
    for step in reversed(range(count.bit_length() - 1)):
        bit = (me >> step) & 1
        other = lax.ppermute(blocks, axis, [(j, j ^ (1 << step)) for j in range(count)])
        first = jnp.where(bit == 1, other, blocks)
        second = jnp.where(bit == 1, blocks, other)
        blocks = jnp.stack([first, second], axis=1).reshape(-1, blocks.shape[1])
    return blocks.reshape(-1)


def power_of_two(count):
    return count & (count - 1) == 0


def silu_slope(value):
    sigma = jax.nn.sigmoid(value)
    return sigma * (1.0 + value * (1.0 - sigma))


def conv(lhs, rhs, dims, padding, strides=(1, 1), rhs_dilation=(1, 1)):
    return lax.conv_general_dilated(
        lhs,
        rhs,
        window_strides=strides,
        padding=padding,
        rhs_dilation=rhs_dilation,
        dimension_numbers=dims,
        preferred_element_type=jnp.float32,
    )


def temporal_apply(hidden, weights, spread):
    return conv(
        hidden,
        weights[:, None],
        ("NHWC", "HWIO", "NHWC"),
        ((spread, spread), (0, 0)),
        rhs_dilation=(spread, 1),
    )


def temporal_transpose(slope_grad, weights, spread):
    flipped = weights[::-1][:, None]
    return conv(
        slope_grad,
        flipped,
        ("NHWC", "HWOI", "NHWC"),
        ((spread, spread), (0, 0)),
        rhs_dilation=(spread, 1),
    )


def temporal_wgrad(hidden, slope_grad, spread):
    out = conv(
        hidden,
        slope_grad,
        ("CHWN", "IHWO", "HWNC"),
        ((spread, spread), (0, 0)),
        strides=(spread, 1),
    )
    return out[:, 0]


def local(clip_pixels, cotangent, master_weights, first_moment, second_moment):
    count = lax.axis_size("pix")
    if power_of_two(count):
        weights_bf = tree_gather(master_weights.astype(jnp.bfloat16), "pix")
    else:
        weights_bf = lax.all_gather(master_weights.astype(jnp.bfloat16), "pix", axis=0, tiled=True)
    split_at = 9 * C * COUT
    spatial_w = weights_bf[:split_at].reshape(3, 3, C, COUT)
    temporal_w = weights_bf[split_at:].reshape(LAYERS, 3, C, C)
    frame_total = clip_pixels.shape[0]
    row_count = clip_pixels.shape[1]
    hidden = clip_pixels.reshape(frame_total // CLEN, CLEN, row_count * W, C)
    inputs = []
    preacts = []
    for layer_index in range(LAYERS):
        spread = 2**layer_index
        inputs.append(hidden)
        preact = temporal_apply(hidden, temporal_w[layer_index], spread)
        preacts.append(preact)
        hidden = (hidden.astype(jnp.float32) + jax.nn.silu(preact)).astype(jnp.bfloat16)
    row_hidden = hidden.reshape(frame_total, row_count, W * C)
    extended = extended_2(row_hidden, (("pix", 1),), 1).reshape(frame_total, row_count + 2, W, C)
    cot_block = cotangent.reshape(frame_total, row_count, W, COUT)
    output = conv(extended, spatial_w, ("NHWC", "HWIO", "NHWC"), ((0, 0), (1, 1)))
    slope_grad = (cot_block.astype(jnp.float32) * silu_slope(output)).astype(jnp.bfloat16)
    grad_spatial = conv(extended, slope_grad, ("CHWN", "IHWO", "HWNC"), ((0, 0), (1, 1)))
    grad_rows = extended_2(
        slope_grad.reshape(frame_total, row_count, W * COUT), (("pix", 1),), 1
    ).reshape(frame_total, row_count + 2, W, COUT)
    row_back = conv(
        grad_rows, spatial_w[::-1, ::-1], ("NHWC", "HWOI", "NHWC"), ((0, 0), (1, 1))
    ).astype(jnp.bfloat16)
    carried_grad = row_back.reshape(frame_total // CLEN, CLEN, row_count * W, C).astype(jnp.float32)
    layer_grads = [None] * LAYERS
    for layer_index in reversed(range(LAYERS)):
        spread = 2**layer_index
        preact = preacts[layer_index]
        slope_grad_t = (carried_grad * silu_slope(preact)).astype(jnp.bfloat16)
        layer_grads[layer_index] = temporal_wgrad(inputs[layer_index], slope_grad_t, spread)
        if layer_index > 0:
            carried_grad = carried_grad + temporal_transpose(
                slope_grad_t, temporal_w[layer_index], spread
            )
    grad_local = jnp.concatenate([grad_spatial.reshape(-1), jnp.stack(layer_grads).reshape(-1)])
    if power_of_two(count):
        grad_share = tree_sum_scatter(grad_local, "pix")
    else:
        grad_share = lax.psum_scatter(grad_local, "pix", scatter_dimension=0, tiled=True)
    moment_one = 0.9 * first_moment + 0.1 * grad_share
    moment_two = 0.95 * second_moment + 0.05 * grad_share * grad_share
    adam_step = moment_one / (jnp.sqrt(moment_two) + 1e-08)
    updated = (master_weights - 0.001 * adam_step).astype(jnp.bfloat16)
    if power_of_two(count):
        new_weights = tree_gather(updated, "pix")
    else:
        new_weights = lax.all_gather(updated, "pix", axis=0, tiled=True)
    return (adam_step, new_weights)


def solution(mesh):
    in_specs = (
        P("parts", "pix", None),
        P("parts", "pix", None),
        P(("parts", "pix")),
        P(("parts", "pix")),
        P(("parts", "pix")),
    )
    out_specs = (P(("parts", "pix")), P("parts"))
    return jax.shard_map(local, mesh=mesh, in_specs=in_specs, out_specs=out_specs, check_vma=False)
```

```python
import jax
import jax.numpy as jnp
from jax import lax
from jax.sharding import PartitionSpec as P

C = 64
COUT = 256
LAYERS = 3
CLEN = 32
W = 16


def extended_2(cells, sides, width):
    for axis, dim in sides:
        count = lax.axis_size(axis)
        ends = count - 1
        head = lax.slice_in_dim(cells, 0, width, axis=dim)
        tail = lax.slice_in_dim(cells, cells.shape[dim] - width, cells.shape[dim], axis=dim)
        cells = jnp.concatenate(
            [
                lax.ppermute(tail, axis, [(i, (i + 1) % count) for i in range(ends)]),
                cells,
                lax.ppermute(head, axis, [((i + 1) % count, i) for i in range(ends)]),
            ],
            axis=dim,
        )
    return cells


def tree_sum_scatter(values, axis):
    count = lax.axis_size(axis)
    me = lax.axis_index(axis)
    blocks = values.reshape(count, -1)
    step = 0
    while (1 << step) < count:
        bit = (me >> step) & 1
        blocks = blocks.reshape(blocks.shape[0] // 2, 2, blocks.shape[1])
        low, high = blocks[:, 0], blocks[:, 1]
        keep = jnp.where(bit == 1, high, low)
        send = jnp.where(bit == 1, low, high)
        blocks = keep + lax.ppermute(send, axis, [(j, j ^ (1 << step)) for j in range(count)])
        step += 1
    return blocks.reshape(-1)


def tree_gather(values, axis):
    count = lax.axis_size(axis)
    me = lax.axis_index(axis)
    blocks = values.reshape(1, -1)
    for step in reversed(range(count.bit_length() - 1)):
        bit = (me >> step) & 1
        other = lax.ppermute(blocks, axis, [(j, j ^ (1 << step)) for j in range(count)])
        first = jnp.where(bit == 1, other, blocks)
        second = jnp.where(bit == 1, blocks, other)
        blocks = jnp.stack([first, second], axis=1).reshape(-1, blocks.shape[1])
    return blocks.reshape(-1)


def power_of_two(count):
    return count & (count - 1) == 0


def silu_slope(value):
    sigma = jax.nn.sigmoid(value)
    return sigma * (1.0 + value * (1.0 - sigma))


def conv(lhs, rhs, dims, padding, strides=(1, 1), rhs_dilation=(1, 1)):
    return lax.conv_general_dilated(
        lhs,
        rhs,
        window_strides=strides,
        padding=padding,
        rhs_dilation=rhs_dilation,
        dimension_numbers=dims,
        preferred_element_type=jnp.float32,
    )


def temporal_columns(values, spread, flip=False):
    length = values.shape[1]
    padded = jnp.pad(values, ((0, 0), (spread, spread), (0, 0), (0, 0)))
    order = (2, 1, 0) if flip else (0, 1, 2)
    cols = jnp.concatenate(
        [padded[:, tap * spread : tap * spread + length] for tap in order], axis=-1
    )
    return cols.reshape(-1, cols.shape[-1])


def matmul(lhs, rhs):
    return jnp.dot(lhs, rhs, preferred_element_type=jnp.float32)


def local(clip_pixels, cotangent, master_weights, first_moment, second_moment):
    count = lax.axis_size("pix")
    if power_of_two(count):
        weights_bf = tree_gather(master_weights.astype(jnp.bfloat16), "pix")
    else:
        weights_bf = lax.all_gather(master_weights.astype(jnp.bfloat16), "pix", axis=0, tiled=True)
    split_at = 9 * C * COUT
    spatial_w = weights_bf[:split_at].reshape(3, 3, C, COUT)
    temporal_w = weights_bf[split_at:].reshape(LAYERS, 3, C, C)
    frame_total = clip_pixels.shape[0]
    row_count = clip_pixels.shape[1]
    hidden = clip_pixels.reshape(frame_total // CLEN, CLEN, row_count * W, C)
    preacts = []
    columns = []
    for layer_index in range(LAYERS):
        spread = 2**layer_index
        cols = temporal_columns(hidden, spread)
        columns.append(cols)
        preact = matmul(cols, temporal_w[layer_index].reshape(3 * C, C)).reshape(hidden.shape)
        preacts.append(preact)
        hidden = (hidden.astype(jnp.float32) + jax.nn.silu(preact)).astype(jnp.bfloat16)
    row_hidden = hidden.reshape(frame_total, row_count, W * C)
    extended = extended_2(row_hidden, (("pix", 1),), 1).reshape(frame_total, row_count + 2, W, C)
    cot_block = cotangent.reshape(frame_total, row_count, W, COUT)
    framed = jnp.pad(extended, ((0, 0), (0, 0), (1, 1), (0, 0)))
    spatial_cols = jnp.concatenate(
        [framed[:, ky : ky + row_count, kx : kx + W] for ky in range(3) for kx in range(3)], axis=-1
    ).reshape(-1, 9 * C)
    output = matmul(spatial_cols, spatial_w.reshape(9 * C, COUT)).reshape(cot_block.shape)
    slope_grad = (cot_block.astype(jnp.float32) * silu_slope(output)).astype(jnp.bfloat16)
    grad_spatial = lax.dot_general(
        spatial_cols,
        slope_grad.reshape(-1, COUT),
        (((0,), (0,)), ((), ())),
        preferred_element_type=jnp.float32,
    )
    grad_rows = extended_2(
        slope_grad.reshape(frame_total, row_count, W * COUT), (("pix", 1),), 1
    ).reshape(frame_total, row_count + 2, W, COUT)
    row_back = conv(
        grad_rows, spatial_w[::-1, ::-1], ("NHWC", "HWOI", "NHWC"), ((0, 0), (1, 1))
    ).astype(jnp.bfloat16)
    carried_grad = row_back.reshape(frame_total // CLEN, CLEN, row_count * W, C).astype(jnp.float32)
    layer_grads = [None] * LAYERS
    for layer_index in reversed(range(LAYERS)):
        spread = 2**layer_index
        preact = preacts[layer_index]
        slope_grad_t = (carried_grad * silu_slope(preact)).astype(jnp.bfloat16)
        layer_grads[layer_index] = lax.dot_general(
            columns[layer_index],
            slope_grad_t.reshape(-1, C),
            (((0,), (0,)), ((), ())),
            preferred_element_type=jnp.float32,
        )
        if layer_index > 0:
            back_w = jnp.swapaxes(temporal_w[layer_index], 1, 2).reshape(3 * C, C)
            carried_grad = carried_grad + matmul(
                temporal_columns(slope_grad_t, spread, flip=True), back_w
            ).reshape(carried_grad.shape)
    grad_local = jnp.concatenate([grad_spatial.reshape(-1), jnp.stack(layer_grads).reshape(-1)])
    if power_of_two(count):
        grad_share = tree_sum_scatter(grad_local, "pix")
    else:
        grad_share = lax.psum_scatter(grad_local, "pix", scatter_dimension=0, tiled=True)
    moment_one = 0.9 * first_moment + 0.1 * grad_share
    moment_two = 0.95 * second_moment + 0.05 * grad_share * grad_share
    adam_step = moment_one / (jnp.sqrt(moment_two) + 1e-08)
    updated = (master_weights - 0.001 * adam_step).astype(jnp.bfloat16)
    if power_of_two(count):
        new_weights = tree_gather(updated, "pix")
    else:
        new_weights = lax.all_gather(updated, "pix", axis=0, tiled=True)
    return (adam_step, new_weights)


def solution(mesh):
    in_specs = (
        P("parts", "pix", None),
        P("parts", "pix", None),
        P(("parts", "pix")),
        P(("parts", "pix")),
        P(("parts", "pix")),
    )
    out_specs = (P(("parts", "pix")), P("parts"))
    return jax.shard_map(local, mesh=mesh, in_specs=in_specs, out_specs=out_specs, check_vma=False)
```

```python
import jax
import jax.numpy as jnp
from jax import lax
from jax.experimental import pallas as pl
from jax.experimental.pallas import tpu as pltpu
from jax.sharding import PartitionSpec as P

C = 64
COUT = 256
LAYERS = 3
CLEN = 32
W = 16


def extended_2(cells, sides, width):
    for axis, dim in sides:
        count = lax.axis_size(axis)
        ends = count - 1
        head = lax.slice_in_dim(cells, 0, width, axis=dim)
        tail = lax.slice_in_dim(cells, cells.shape[dim] - width, cells.shape[dim], axis=dim)
        cells = jnp.concatenate(
            [
                lax.ppermute(tail, axis, [(i, (i + 1) % count) for i in range(ends)]),
                cells,
                lax.ppermute(head, axis, [((i + 1) % count, i) for i in range(ends)]),
            ],
            axis=dim,
        )
    return cells


def tree_sum_scatter(values, axis):
    count = lax.axis_size(axis)
    me = lax.axis_index(axis)
    blocks = values.reshape(count, -1)
    step = 0
    while (1 << step) < count:
        bit = (me >> step) & 1
        blocks = blocks.reshape(blocks.shape[0] // 2, 2, blocks.shape[1])
        low, high = blocks[:, 0], blocks[:, 1]
        keep = jnp.where(bit == 1, high, low)
        send = jnp.where(bit == 1, low, high)
        blocks = keep + lax.ppermute(send, axis, [(j, j ^ (1 << step)) for j in range(count)])
        step += 1
    return blocks.reshape(-1)


def tree_gather(values, axis):
    count = lax.axis_size(axis)
    me = lax.axis_index(axis)
    blocks = values.reshape(1, -1)
    for step in reversed(range(count.bit_length() - 1)):
        bit = (me >> step) & 1
        other = lax.ppermute(blocks, axis, [(j, j ^ (1 << step)) for j in range(count)])
        first = jnp.where(bit == 1, other, blocks)
        second = jnp.where(bit == 1, blocks, other)
        blocks = jnp.stack([first, second], axis=1).reshape(-1, blocks.shape[1])
    return blocks.reshape(-1)


def power_of_two(count):
    return count & (count - 1) == 0


def silu_slope(value):
    sigma = jax.nn.sigmoid(value)
    return sigma * (1.0 + value * (1.0 - sigma))


def conv(lhs, rhs, dims, padding, strides=(1, 1), rhs_dilation=(1, 1)):
    return lax.conv_general_dilated(
        lhs,
        rhs,
        window_strides=strides,
        padding=padding,
        rhs_dilation=rhs_dilation,
        dimension_numbers=dims,
        preferred_element_type=jnp.float32,
    )


def temporal_columns(values, spread, flip=False):
    length = values.shape[1]
    padded = jnp.pad(values, ((0, 0), (spread, spread), (0, 0), (0, 0)))
    order = (2, 1, 0) if flip else (0, 1, 2)
    cols = jnp.concatenate(
        [padded[:, tap * spread : tap * spread + length] for tap in order], axis=-1
    )
    return cols.reshape(-1, cols.shape[-1])


def matmul(lhs, rhs):
    return jnp.dot(lhs, rhs, preferred_element_type=jnp.float32)


def spatial_kernel(cols_ref, w_ref, cot_ref, dy_ref, g_ref):
    cols = cols_ref[...]
    y = jnp.dot(cols, w_ref[...], preferred_element_type=jnp.float32)
    s = 1.0 / (1.0 + jnp.exp(-y))
    dy = (cot_ref[...].astype(jnp.float32) * (s * (1.0 + y * (1.0 - s)))).astype(jnp.bfloat16)
    dy_ref[...] = dy
    part = lax.dot_general(cols, dy, (((0,), (0,)), ((), ())), preferred_element_type=jnp.float32)
    @pl.when(pl.program_id(0) == 0)
    def _():
        g_ref[...] = part
    @pl.when(pl.program_id(0) > 0)
    def _():
        g_ref[...] += part

def spatial_call(cols, wmat, cot, block=1024):
    rows, k = cols.shape
    n = wmat.shape[1]
    return pl.pallas_call(
        spatial_kernel,
        grid=(rows // block,),
        in_specs=[pl.BlockSpec((block, k), lambda i: (i, 0)), pl.BlockSpec((k, n), lambda i: (0, 0)), pl.BlockSpec((block, n), lambda i: (i, 0))],
        out_specs=[pl.BlockSpec((block, n), lambda i: (i, 0)), pl.BlockSpec((k, n), lambda i: (0, 0))],
        out_shape=[jax.ShapeDtypeStruct((rows, n), jnp.bfloat16), jax.ShapeDtypeStruct((k, n), jnp.float32)],
        compiler_params=pltpu.CompilerParams(dimension_semantics=("arbitrary",)),
        cost_estimate=pl.CostEstimate(flops=4 * rows * k * n, transcendentals=rows * n, bytes_accessed=2 * rows * (k + 2 * n) + 4 * k * n),
    )(cols, wmat, cot)


def local(clip_pixels, cotangent, master_weights, first_moment, second_moment):
    count = lax.axis_size("pix")
    if power_of_two(count):
        weights_bf = tree_gather(master_weights.astype(jnp.bfloat16), "pix")
    else:
        weights_bf = lax.all_gather(master_weights.astype(jnp.bfloat16), "pix", axis=0, tiled=True)
    split_at = 9 * C * COUT
    spatial_w = weights_bf[:split_at].reshape(3, 3, C, COUT)
    temporal_w = weights_bf[split_at:].reshape(LAYERS, 3, C, C)
    frame_total = clip_pixels.shape[0]
    row_count = clip_pixels.shape[1]
    hidden = clip_pixels.reshape(frame_total // CLEN, CLEN, row_count * W, C)
    preacts = []
    columns = []
    for layer_index in range(LAYERS):
        spread = 2**layer_index
        cols = temporal_columns(hidden, spread)
        columns.append(cols)
        preact = matmul(cols, temporal_w[layer_index].reshape(3 * C, C)).reshape(hidden.shape)
        preacts.append(preact)
        hidden = (hidden.astype(jnp.float32) + jax.nn.silu(preact)).astype(jnp.bfloat16)
    row_hidden = hidden.reshape(frame_total, row_count, W * C)
    extended = extended_2(row_hidden, (("pix", 1),), 1).reshape(frame_total, row_count + 2, W, C)
    cot_block = cotangent.reshape(frame_total, row_count, W, COUT)
    framed = jnp.pad(extended, ((0, 0), (0, 0), (1, 1), (0, 0)))
    spatial_cols = jnp.concatenate(
        [framed[:, ky : ky + row_count, kx : kx + W] for ky in range(3) for kx in range(3)], axis=-1
    ).reshape(-1, 9 * C)
    rows = spatial_cols.shape[0]
    slope_grad, grad_spatial = spatial_call(
        spatial_cols,
        spatial_w.reshape(9 * C, COUT),
        cotangent.reshape(rows, COUT),
        block=1024 if rows % 1024 == 0 else rows,
    )
    slope_grad = slope_grad.reshape(cot_block.shape)
    grad_rows = extended_2(
        slope_grad.reshape(frame_total, row_count, W * COUT), (("pix", 1),), 1
    ).reshape(frame_total, row_count + 2, W, COUT)
    stacked = grad_rows.reshape(1, frame_total * (row_count + 2), W, COUT)
    row_back = conv(
        stacked, spatial_w[::-1, ::-1], ("NHWC", "HWOI", "NHWC"), ((0, 0), (1, 1))
    )
    row_back = jnp.pad(row_back, ((0, 0), (0, 2), (0, 0), (0, 0))).reshape(
        frame_total, row_count + 2, W, C
    )[:, :row_count].astype(jnp.bfloat16)
    carried_grad = row_back.reshape(frame_total // CLEN, CLEN, row_count * W, C).astype(jnp.float32)
    layer_grads = [None] * LAYERS
    for layer_index in reversed(range(LAYERS)):
        spread = 2**layer_index
        preact = preacts[layer_index]
        slope_grad_t = (carried_grad * silu_slope(preact)).astype(jnp.bfloat16)
        layer_grads[layer_index] = lax.dot_general(
            columns[layer_index],
            slope_grad_t.reshape(-1, C),
            (((0,), (0,)), ((), ())),
            preferred_element_type=jnp.float32,
        )
        if layer_index > 0:
            back_w = jnp.swapaxes(temporal_w[layer_index], 1, 2).reshape(3 * C, C)
            carried_grad = carried_grad + matmul(
                temporal_columns(slope_grad_t, spread, flip=True), back_w
            ).reshape(carried_grad.shape)
    grad_local = jnp.concatenate([grad_spatial.reshape(-1), jnp.stack(layer_grads).reshape(-1)])
    if power_of_two(count):
        grad_share = tree_sum_scatter(grad_local, "pix")
    else:
        grad_share = lax.psum_scatter(grad_local, "pix", scatter_dimension=0, tiled=True)
    moment_one = 0.9 * first_moment + 0.1 * grad_share
    moment_two = 0.95 * second_moment + 0.05 * grad_share * grad_share
    adam_step = moment_one / (jnp.sqrt(moment_two) + 1e-08)
    updated = (master_weights - 0.001 * adam_step).astype(jnp.bfloat16)
    if power_of_two(count):
        new_weights = tree_gather(updated, "pix")
    else:
        new_weights = lax.all_gather(updated, "pix", axis=0, tiled=True)
    return (adam_step, new_weights)


def solution(mesh):
    in_specs = (
        P("parts", "pix", None),
        P("parts", "pix", None),
        P(("parts", "pix")),
        P(("parts", "pix")),
        P(("parts", "pix")),
    )
    out_specs = (P(("parts", "pix")), P("parts"))
    return jax.shard_map(local, mesh=mesh, in_specs=in_specs, out_specs=out_specs, check_vma=False)
```

```python
import jax
import jax.numpy as jnp
from jax import lax
from jax.experimental.layout import Layout, with_layout_constraint
from jax.sharding import PartitionSpec as P

C = 64
COUT = 256
LAYERS = 3
CLEN = 32
W = 16


def extended_2(cells, sides, width):
    for axis, dim in sides:
        count = lax.axis_size(axis)
        ends = count - 1
        head = lax.slice_in_dim(cells, 0, width, axis=dim)
        tail = lax.slice_in_dim(cells, cells.shape[dim] - width, cells.shape[dim], axis=dim)
        cells = jnp.concatenate(
            [
                lax.ppermute(tail, axis, [(i, (i + 1) % count) for i in range(ends)]),
                cells,
                lax.ppermute(head, axis, [((i + 1) % count, i) for i in range(ends)]),
            ],
            axis=dim,
        )
    return cells


def tree_sum_scatter(values, axis):
    count = lax.axis_size(axis)
    me = lax.axis_index(axis)
    blocks = values.reshape(count, -1)
    step = 0
    while (1 << step) < count:
        bit = (me >> step) & 1
        blocks = blocks.reshape(blocks.shape[0] // 2, 2, blocks.shape[1])
        low, high = blocks[:, 0], blocks[:, 1]
        keep = jnp.where(bit == 1, high, low)
        send = jnp.where(bit == 1, low, high)
        blocks = keep + lax.ppermute(send, axis, [(j, j ^ (1 << step)) for j in range(count)])
        step += 1
    return blocks.reshape(-1)


def tree_gather(values, axis):
    count = lax.axis_size(axis)
    me = lax.axis_index(axis)
    blocks = values.reshape(1, -1)
    for step in reversed(range(count.bit_length() - 1)):
        bit = (me >> step) & 1
        other = lax.ppermute(blocks, axis, [(j, j ^ (1 << step)) for j in range(count)])
        first = jnp.where(bit == 1, other, blocks)
        second = jnp.where(bit == 1, blocks, other)
        blocks = jnp.stack([first, second], axis=1).reshape(-1, blocks.shape[1])
    return blocks.reshape(-1)


def power_of_two(count):
    return count & (count - 1) == 0


def silu_slope(value):
    sigma = jax.nn.sigmoid(value)
    return sigma * (1.0 + value * (1.0 - sigma))


def conv(lhs, rhs, dims, padding, strides=(1, 1), rhs_dilation=(1, 1)):
    return lax.conv_general_dilated(
        lhs,
        rhs,
        window_strides=strides,
        padding=padding,
        rhs_dilation=rhs_dilation,
        dimension_numbers=dims,
        preferred_element_type=jnp.float32,
    )


def temporal_columns(values, spread, flip=False):
    length = values.shape[1]
    padded = jnp.pad(values, ((0, 0), (spread, spread), (0, 0), (0, 0)))
    order = (2, 1, 0) if flip else (0, 1, 2)
    cols = jnp.concatenate(
        [padded[:, tap * spread : tap * spread + length] for tap in order], axis=-1
    )
    return cols.reshape(-1, cols.shape[-1])


def row_major(x):
    return with_layout_constraint(x, Layout(tuple(range(x.ndim))))


def matmul(lhs, rhs):
    return jnp.dot(lhs, rhs, preferred_element_type=jnp.float32)


def local(clip_pixels, cotangent, master_weights, first_moment, second_moment):
    count = lax.axis_size("pix")
    if power_of_two(count):
        weights_bf = tree_gather(master_weights.astype(jnp.bfloat16), "pix")
    else:
        weights_bf = lax.all_gather(master_weights.astype(jnp.bfloat16), "pix", axis=0, tiled=True)
    split_at = 9 * C * COUT
    spatial_w = weights_bf[:split_at].reshape(3, 3, C, COUT)
    temporal_w = weights_bf[split_at:].reshape(LAYERS, 3, C, C)
    frame_total = clip_pixels.shape[0]
    row_count = clip_pixels.shape[1]
    hidden = clip_pixels.reshape(frame_total // CLEN, CLEN, row_count * W, C)
    preacts = []
    columns = []
    for layer_index in range(LAYERS):
        spread = 2**layer_index
        cols = temporal_columns(hidden, spread)
        columns.append(cols)
        preact = matmul(cols, temporal_w[layer_index].reshape(3 * C, C)).reshape(hidden.shape)
        preacts.append(preact)
        hidden = (hidden.astype(jnp.float32) + jax.nn.silu(preact)).astype(jnp.bfloat16)
    row_hidden = hidden.reshape(frame_total, row_count, W * C)
    extended = extended_2(row_hidden, (("pix", 1),), 1).reshape(frame_total, row_count + 2, W, C)
    cot_block = cotangent.reshape(frame_total, row_count, W, COUT)
    framed = jnp.pad(extended, ((0, 0), (0, 0), (1, 1), (0, 0)))
    spatial_cols = jnp.concatenate(
        [framed[:, ky : ky + row_count, kx : kx + W] for ky in range(3) for kx in range(3)], axis=-1
    ).reshape(-1, 9 * C)
    spatial_cols = row_major(spatial_cols)
    output = row_major(matmul(spatial_cols, spatial_w.reshape(9 * C, COUT)))
    slope_grad = row_major(
        (row_major(cotangent.reshape(-1, COUT)).astype(jnp.float32) * silu_slope(output)).astype(
            jnp.bfloat16
        )
    )
    grad_spatial = lax.dot_general(
        spatial_cols,
        slope_grad,
        (((0,), (0,)), ((), ())),
        preferred_element_type=jnp.float32,
    )
    grad_rows = extended_2(
        row_major(slope_grad.reshape(frame_total, row_count, W * COUT)), (("pix", 1),), 1
    ).reshape(frame_total, row_count + 2, W, COUT)
    taps = matmul(
        grad_rows.reshape(-1, COUT), jnp.transpose(spatial_w, (3, 0, 1, 2)).reshape(COUT, 9 * C)
    ).reshape(frame_total, row_count + 2, W, 9, C)
    taps = jnp.pad(taps, ((0, 0), (0, 0), (1, 1), (0, 0), (0, 0)))
    row_back = sum(
        taps[:, 2 - ky : 2 - ky + row_count, 2 - kx : 2 - kx + W, 3 * ky + kx]
        for ky in range(3)
        for kx in range(3)
    ).astype(jnp.bfloat16)
    carried_grad = row_back.reshape(frame_total // CLEN, CLEN, row_count * W, C).astype(jnp.float32)
    layer_grads = [None] * LAYERS
    for layer_index in reversed(range(LAYERS)):
        spread = 2**layer_index
        preact = preacts[layer_index]
        slope_grad_t = (carried_grad * silu_slope(preact)).astype(jnp.bfloat16)
        layer_grads[layer_index] = lax.dot_general(
            columns[layer_index],
            slope_grad_t.reshape(-1, C),
            (((0,), (0,)), ((), ())),
            preferred_element_type=jnp.float32,
        )
        if layer_index > 0:
            back_w = jnp.swapaxes(temporal_w[layer_index], 1, 2).reshape(3 * C, C)
            carried_grad = carried_grad + matmul(
                temporal_columns(slope_grad_t, spread, flip=True), back_w
            ).reshape(carried_grad.shape)
    grad_local = jnp.concatenate([grad_spatial.reshape(-1), jnp.stack(layer_grads).reshape(-1)])
    if power_of_two(count):
        grad_share = tree_sum_scatter(grad_local, "pix")
    else:
        grad_share = lax.psum_scatter(grad_local, "pix", scatter_dimension=0, tiled=True)
    moment_one = 0.9 * first_moment + 0.1 * grad_share
    moment_two = 0.95 * second_moment + 0.05 * grad_share * grad_share
    adam_step = moment_one / (jnp.sqrt(moment_two) + 1e-08)
    updated = (master_weights - 0.001 * adam_step).astype(jnp.bfloat16)
    if power_of_two(count):
        new_weights = tree_gather(updated, "pix")
    else:
        new_weights = lax.all_gather(updated, "pix", axis=0, tiled=True)
    return (adam_step, new_weights)


def solution(mesh):
    in_specs = (
        P("parts", "pix", None),
        P("parts", "pix", None),
        P(("parts", "pix")),
        P(("parts", "pix")),
        P(("parts", "pix")),
    )
    out_specs = (P(("parts", "pix")), P("parts"))
    return jax.shard_map(local, mesh=mesh, in_specs=in_specs, out_specs=out_specs, check_vma=False)
```

```python
import jax
import jax.numpy as jnp
from jax import lax
from jax.sharding import PartitionSpec as P

C = 64
COUT = 256
LAYERS = 3
CLEN = 32
W = 16


def extended_2(cells, sides, width):
    for axis, dim in sides:
        count = lax.axis_size(axis)
        ends = count - 1
        head = lax.slice_in_dim(cells, 0, width, axis=dim)
        tail = lax.slice_in_dim(cells, cells.shape[dim] - width, cells.shape[dim], axis=dim)
        cells = jnp.concatenate(
            [
                lax.ppermute(tail, axis, [(i, (i + 1) % count) for i in range(ends)]),
                cells,
                lax.ppermute(head, axis, [((i + 1) % count, i) for i in range(ends)]),
            ],
            axis=dim,
        )
    return cells


def bit_groups(count):
    bits = count.bit_length() - 1
    return [(low, min(2, bits - low)) for low in range(0, bits, 2)]


def partners(count, low, offset):
    return [(j, j ^ (offset << low)) for j in range(count)]


def tree_sum_scatter(values, axis):
    count = lax.axis_size(axis)
    me = lax.axis_index(axis)
    blocks = values.reshape(count, -1)
    for low, width in bit_groups(count):
        size = 1 << width
        mine = (me >> low) & (size - 1)
        parts = blocks.reshape(blocks.shape[0] // size, size, blocks.shape[1])
        total = lax.dynamic_index_in_dim(parts, mine, axis=1, keepdims=False)
        for offset in range(1, size):
            send = lax.dynamic_index_in_dim(parts, mine ^ offset, axis=1, keepdims=False)
            total = total + lax.ppermute(send, axis, partners(count, low, offset))
        blocks = total
    return blocks.reshape(-1)


def tree_gather(values, axis):
    count = lax.axis_size(axis)
    me = lax.axis_index(axis)
    blocks = values.reshape(1, -1)
    for low, width in reversed(bit_groups(count)):
        size = 1 << width
        mine = (me >> low) & (size - 1)
        got = [blocks] + [
            lax.ppermute(blocks, axis, partners(count, low, offset)) for offset in range(1, size)
        ]
        stacked = jnp.stack(got)
        blocks = jnp.stack(
            [lax.dynamic_index_in_dim(stacked, part ^ mine, axis=0, keepdims=False) for part in range(size)],
            axis=1,
        ).reshape(-1, blocks.shape[1])
    return blocks.reshape(-1)


def power_of_two(count):
    return count & (count - 1) == 0


def silu_slope(value):
    sigma = jax.nn.sigmoid(value)
    return sigma * (1.0 + value * (1.0 - sigma))


def conv(lhs, rhs, dims, padding, strides=(1, 1), rhs_dilation=(1, 1)):
    return lax.conv_general_dilated(
        lhs,
        rhs,
        window_strides=strides,
        padding=padding,
        rhs_dilation=rhs_dilation,
        dimension_numbers=dims,
        preferred_element_type=jnp.float32,
    )


def temporal_columns(values, spread, flip=False):
    length = values.shape[1]
    padded = jnp.pad(values, ((0, 0), (spread, spread), (0, 0), (0, 0)))
    order = (2, 1, 0) if flip else (0, 1, 2)
    cols = jnp.concatenate(
        [padded[:, tap * spread : tap * spread + length] for tap in order], axis=-1
    )
    return cols.reshape(-1, cols.shape[-1])


def matmul(lhs, rhs):
    return jnp.dot(lhs, rhs, preferred_element_type=jnp.float32)


def local(clip_pixels, cotangent, master_weights, first_moment, second_moment):
    count = lax.axis_size("pix")
    if power_of_two(count):
        weights_bf = tree_gather(master_weights.astype(jnp.bfloat16), "pix")
    else:
        weights_bf = lax.all_gather(master_weights.astype(jnp.bfloat16), "pix", axis=0, tiled=True)
    split_at = 9 * C * COUT
    spatial_w = weights_bf[:split_at].reshape(3, 3, C, COUT)
    temporal_w = weights_bf[split_at:].reshape(LAYERS, 3, C, C)
    frame_total = clip_pixels.shape[0]
    row_count = clip_pixels.shape[1]
    hidden = clip_pixels.reshape(frame_total // CLEN, CLEN, row_count * W, C)
    preacts = []
    columns = []
    for layer_index in range(LAYERS):
        spread = 2**layer_index
        cols = temporal_columns(hidden, spread)
        columns.append(cols)
        preact = matmul(cols, temporal_w[layer_index].reshape(3 * C, C)).reshape(hidden.shape)
        preacts.append(preact)
        hidden = (hidden.astype(jnp.float32) + jax.nn.silu(preact)).astype(jnp.bfloat16)
    row_hidden = hidden.reshape(frame_total, row_count, W * C)
    extended = extended_2(row_hidden, (("pix", 1),), 1).reshape(frame_total, row_count + 2, W, C)
    cot_block = cotangent.reshape(frame_total, row_count, W, COUT)
    framed = jnp.pad(extended, ((0, 0), (0, 0), (1, 1), (0, 0)))
    spatial_cols = jnp.concatenate(
        [framed[:, ky : ky + row_count, kx : kx + W] for ky in range(3) for kx in range(3)], axis=-1
    ).reshape(-1, 9 * C)
    output = matmul(spatial_cols, spatial_w.reshape(9 * C, COUT)).reshape(cot_block.shape)
    slope_grad = (cot_block.astype(jnp.float32) * silu_slope(output)).astype(jnp.bfloat16)
    grad_spatial = lax.dot_general(
        spatial_cols,
        slope_grad.reshape(-1, COUT),
        (((0,), (0,)), ((), ())),
        preferred_element_type=jnp.float32,
    )
    grad_rows = extended_2(
        slope_grad.reshape(frame_total, row_count, W * COUT), (("pix", 1),), 1
    ).reshape(frame_total, row_count + 2, W, COUT)
    row_back = conv(
        grad_rows, spatial_w[::-1, ::-1], ("NHWC", "HWOI", "NHWC"), ((0, 0), (1, 1))
    ).astype(jnp.bfloat16)
    carried_grad = row_back.reshape(frame_total // CLEN, CLEN, row_count * W, C).astype(jnp.float32)
    layer_grads = [None] * LAYERS
    for layer_index in reversed(range(LAYERS)):
        spread = 2**layer_index
        preact = preacts[layer_index]
        slope_grad_t = (carried_grad * silu_slope(preact)).astype(jnp.bfloat16)
        layer_grads[layer_index] = lax.dot_general(
            columns[layer_index],
            slope_grad_t.reshape(-1, C),
            (((0,), (0,)), ((), ())),
            preferred_element_type=jnp.float32,
        )
        if layer_index > 0:
            back_w = jnp.swapaxes(temporal_w[layer_index], 1, 2).reshape(3 * C, C)
            carried_grad = carried_grad + matmul(
                temporal_columns(slope_grad_t, spread, flip=True), back_w
            ).reshape(carried_grad.shape)
    grad_local = jnp.concatenate([grad_spatial.reshape(-1), jnp.stack(layer_grads).reshape(-1)])
    if power_of_two(count):
        grad_share = tree_sum_scatter(grad_local, "pix")
    else:
        grad_share = lax.psum_scatter(grad_local, "pix", scatter_dimension=0, tiled=True)
    moment_one = 0.9 * first_moment + 0.1 * grad_share
    moment_two = 0.95 * second_moment + 0.05 * grad_share * grad_share
    adam_step = moment_one / (jnp.sqrt(moment_two) + 1e-08)
    updated = (master_weights - 0.001 * adam_step).astype(jnp.bfloat16)
    if power_of_two(count):
        new_weights = tree_gather(updated, "pix")
    else:
        new_weights = lax.all_gather(updated, "pix", axis=0, tiled=True)
    return (adam_step, new_weights)


def solution(mesh):
    in_specs = (
        P("parts", "pix", None),
        P("parts", "pix", None),
        P(("parts", "pix")),
        P(("parts", "pix")),
        P(("parts", "pix")),
    )
    out_specs = (P(("parts", "pix")), P("parts"))
    return jax.shard_map(local, mesh=mesh, in_specs=in_specs, out_specs=out_specs, check_vma=False)
```

```python
import jax
import jax.numpy as jnp
from jax import lax
from jax.sharding import PartitionSpec as P

C = 64
COUT = 256
LAYERS = 3
CLEN = 32
W = 16


def extended_2(cells, sides, width):
    for axis, dim in sides:
        count = lax.axis_size(axis)
        ends = count - 1
        head = lax.slice_in_dim(cells, 0, width, axis=dim)
        tail = lax.slice_in_dim(cells, cells.shape[dim] - width, cells.shape[dim], axis=dim)
        cells = jnp.concatenate(
            [
                lax.ppermute(tail, axis, [(i, (i + 1) % count) for i in range(ends)]),
                cells,
                lax.ppermute(head, axis, [((i + 1) % count, i) for i in range(ends)]),
            ],
            axis=dim,
        )
    return cells


def bit_groups(count):
    bits = count.bit_length() - 1
    return [(low, min(2, bits - low)) for low in range(0, bits, 2)]


def partners(count, low, offset):
    return [(j, j ^ (offset << low)) for j in range(count)]


def tree_sum_scatter(values, axis):
    count = lax.axis_size(axis)
    me = lax.axis_index(axis)
    blocks = values.reshape(count, -1)
    for low, width in bit_groups(count):
        size = 1 << width
        mine = (me >> low) & (size - 1)
        parts = blocks.reshape(blocks.shape[0] // size, size, blocks.shape[1])
        total = lax.dynamic_index_in_dim(parts, mine, axis=1, keepdims=False)
        for offset in range(1, size):
            send = lax.dynamic_index_in_dim(parts, mine ^ offset, axis=1, keepdims=False)
            total = total + lax.ppermute(send, axis, partners(count, low, offset))
        blocks = total
    return blocks.reshape(-1)


def tree_gather(values, axis):
    count = lax.axis_size(axis)
    me = lax.axis_index(axis)
    blocks = values.reshape(1, -1)
    for low, width in reversed(bit_groups(count)):
        size = 1 << width
        mine = (me >> low) & (size - 1)
        got = [blocks] + [
            lax.ppermute(blocks, axis, partners(count, low, offset)) for offset in range(1, size)
        ]
        stacked = jnp.stack(got)
        blocks = jnp.stack(
            [lax.dynamic_index_in_dim(stacked, part ^ mine, axis=0, keepdims=False) for part in range(size)],
            axis=1,
        ).reshape(-1, blocks.shape[1])
    return blocks.reshape(-1)


def power_of_two(count):
    return count & (count - 1) == 0


def silu_slope(value):
    sigma = jax.nn.sigmoid(value)
    return sigma * (1.0 + value * (1.0 - sigma))


def conv(lhs, rhs, dims, padding, strides=(1, 1), rhs_dilation=(1, 1)):
    return lax.conv_general_dilated(
        lhs,
        rhs,
        window_strides=strides,
        padding=padding,
        rhs_dilation=rhs_dilation,
        dimension_numbers=dims,
        preferred_element_type=jnp.float32,
    )


def temporal_columns(values, spread, flip=False):
    length = values.shape[1]
    padded = jnp.pad(values, ((0, 0), (spread, spread), (0, 0), (0, 0)))
    order = (2, 1, 0) if flip else (0, 1, 2)
    cols = jnp.concatenate(
        [padded[:, tap * spread : tap * spread + length] for tap in order], axis=-1
    )
    return cols.reshape(-1, cols.shape[-1])


def matmul(lhs, rhs):
    return jnp.dot(lhs, rhs, preferred_element_type=jnp.float32)


def local(clip_pixels, cotangent, master_weights, first_moment, second_moment):
    count = lax.axis_size("pix")
    if power_of_two(count):
        weights_bf = tree_gather(master_weights.astype(jnp.bfloat16), "pix")
    else:
        weights_bf = lax.all_gather(master_weights.astype(jnp.bfloat16), "pix", axis=0, tiled=True)
    split_at = 9 * C * COUT
    spatial_w = weights_bf[:split_at].reshape(3, 3, C, COUT)
    temporal_w = weights_bf[split_at:].reshape(LAYERS, 3, C, C)
    frame_total = clip_pixels.shape[0]
    row_count = clip_pixels.shape[1]
    hidden = clip_pixels.reshape(frame_total // CLEN, CLEN, row_count * W, C)
    preacts = []
    columns = []
    for layer_index in range(LAYERS):
        spread = 2**layer_index
        cols = temporal_columns(hidden, spread)
        columns.append(cols)
        preact = matmul(cols, temporal_w[layer_index].reshape(3 * C, C)).reshape(hidden.shape)
        preacts.append(preact)
        hidden = (hidden.astype(jnp.float32) + jax.nn.silu(preact)).astype(jnp.bfloat16)
    cot_rows = extended_2(cotangent, (("pix", 1),), 1).reshape(frame_total, row_count + 2, W, COUT)
    row_hidden = hidden.reshape(frame_total, row_count, W * C)
    extended = extended_2(row_hidden, (("pix", 1),), 2).reshape(frame_total, row_count + 4, W, C)
    framed = jnp.pad(extended, ((0, 0), (0, 0), (1, 1), (0, 0)))
    spatial_cols = jnp.concatenate(
        [framed[:, ky : ky + row_count + 2, kx : kx + W] for ky in range(3) for kx in range(3)],
        axis=-1,
    )
    output = matmul(spatial_cols.reshape(-1, 9 * C), spatial_w.reshape(9 * C, COUT)).reshape(
        cot_rows.shape
    )
    grad_rows = (cot_rows.astype(jnp.float32) * silu_slope(output)).astype(jnp.bfloat16)
    grad_spatial = lax.dot_general(
        spatial_cols[:, 1 : row_count + 1].reshape(-1, 9 * C),
        grad_rows[:, 1 : row_count + 1].reshape(-1, COUT),
        (((0,), (0,)), ((), ())),
        preferred_element_type=jnp.float32,
    )
    row_back = conv(
        grad_rows, spatial_w[::-1, ::-1], ("NHWC", "HWOI", "NHWC"), ((0, 0), (1, 1))
    ).astype(jnp.bfloat16)
    carried_grad = row_back.reshape(frame_total // CLEN, CLEN, row_count * W, C).astype(jnp.float32)
    layer_grads = [None] * LAYERS
    for layer_index in reversed(range(LAYERS)):
        spread = 2**layer_index
        preact = preacts[layer_index]
        slope_grad_t = (carried_grad * silu_slope(preact)).astype(jnp.bfloat16)
        layer_grads[layer_index] = lax.dot_general(
            columns[layer_index],
            slope_grad_t.reshape(-1, C),
            (((0,), (0,)), ((), ())),
            preferred_element_type=jnp.float32,
        )
        if layer_index > 0:
            back_w = jnp.swapaxes(temporal_w[layer_index], 1, 2).reshape(3 * C, C)
            carried_grad = carried_grad + matmul(
                temporal_columns(slope_grad_t, spread, flip=True), back_w
            ).reshape(carried_grad.shape)
    grad_local = jnp.concatenate([grad_spatial.reshape(-1), jnp.stack(layer_grads).reshape(-1)])
    if power_of_two(count):
        grad_share = tree_sum_scatter(grad_local, "pix")
    else:
        grad_share = lax.psum_scatter(grad_local, "pix", scatter_dimension=0, tiled=True)
    moment_one = 0.9 * first_moment + 0.1 * grad_share
    moment_two = 0.95 * second_moment + 0.05 * grad_share * grad_share
    adam_step = moment_one / (jnp.sqrt(moment_two) + 1e-08)
    updated = (master_weights - 0.001 * adam_step).astype(jnp.bfloat16)
    if power_of_two(count):
        new_weights = tree_gather(updated, "pix")
    else:
        new_weights = lax.all_gather(updated, "pix", axis=0, tiled=True)
    return (adam_step, new_weights)


def solution(mesh):
    in_specs = (
        P("parts", "pix", None),
        P("parts", "pix", None),
        P(("parts", "pix")),
        P(("parts", "pix")),
        P(("parts", "pix")),
    )
    out_specs = (P(("parts", "pix")), P("parts"))
    return jax.shard_map(local, mesh=mesh, in_specs=in_specs, out_specs=out_specs, check_vma=False)
```

```python
import jax
import jax.numpy as jnp
from jax import lax
from jax.sharding import PartitionSpec as P

C = 64
COUT = 256
LAYERS = 3
CLEN = 32
W = 16


def extended_2(cells, sides, width):
    for axis, dim in sides:
        count = lax.axis_size(axis)
        ends = count - 1
        head = lax.slice_in_dim(cells, 0, width, axis=dim)
        tail = lax.slice_in_dim(cells, cells.shape[dim] - width, cells.shape[dim], axis=dim)
        cells = jnp.concatenate(
            [
                lax.ppermute(tail, axis, [(i, (i + 1) % count) for i in range(ends)]),
                cells,
                lax.ppermute(head, axis, [((i + 1) % count, i) for i in range(ends)]),
            ],
            axis=dim,
        )
    return cells


def bit_groups(count):
    bits = count.bit_length() - 1
    return [(low, min(2, bits - low)) for low in range(0, bits, 2)]


def partners(count, low, offset):
    return [(j, j ^ (offset << low)) for j in range(count)]


def tree_sum_scatter(values, axis):
    count = lax.axis_size(axis)
    me = lax.axis_index(axis)
    blocks = values.reshape(count, -1)
    for low, width in bit_groups(count):
        size = 1 << width
        mine = (me >> low) & (size - 1)
        parts = blocks.reshape(blocks.shape[0] // size, size, blocks.shape[1])
        total = lax.dynamic_index_in_dim(parts, mine, axis=1, keepdims=False)
        for offset in range(1, size):
            send = lax.dynamic_index_in_dim(parts, mine ^ offset, axis=1, keepdims=False)
            total = total + lax.ppermute(send, axis, partners(count, low, offset))
        blocks = total
    return blocks.reshape(-1)


def tree_gather(values, axis):
    count = lax.axis_size(axis)
    me = lax.axis_index(axis)
    blocks = values.reshape(1, -1)
    for low, width in reversed(bit_groups(count)):
        size = 1 << width
        mine = (me >> low) & (size - 1)
        got = [blocks] + [
            lax.ppermute(blocks, axis, partners(count, low, offset)) for offset in range(1, size)
        ]
        stacked = jnp.stack(got)
        blocks = jnp.stack(
            [lax.dynamic_index_in_dim(stacked, part ^ mine, axis=0, keepdims=False) for part in range(size)],
            axis=1,
        ).reshape(-1, blocks.shape[1])
    return blocks.reshape(-1)


def power_of_two(count):
    return count & (count - 1) == 0


def silu_slope(value):
    sigma = jax.nn.sigmoid(value)
    return sigma * (1.0 + value * (1.0 - sigma))


def conv(lhs, rhs, dims, padding, strides=(1, 1), rhs_dilation=(1, 1)):
    return lax.conv_general_dilated(
        lhs,
        rhs,
        window_strides=strides,
        padding=padding,
        rhs_dilation=rhs_dilation,
        dimension_numbers=dims,
        preferred_element_type=jnp.float32,
    )


def temporal_columns(values, spread, flip=False):
    length = values.shape[1]
    padded = jnp.pad(values, ((0, 0), (spread, spread), (0, 0), (0, 0)))
    order = (2, 1, 0) if flip else (0, 1, 2)
    cols = jnp.concatenate(
        [padded[:, tap * spread : tap * spread + length] for tap in order], axis=-1
    )
    return cols.reshape(-1, cols.shape[-1])


def matmul(lhs, rhs):
    return jnp.dot(lhs, rhs, preferred_element_type=jnp.float32)


def local(clip_pixels, cotangent, master_weights, first_moment, second_moment):
    count = lax.axis_size("pix")
    if power_of_two(count):
        weights_bf = tree_gather(master_weights.astype(jnp.bfloat16), "pix")
    else:
        weights_bf = lax.all_gather(master_weights.astype(jnp.bfloat16), "pix", axis=0, tiled=True)
    split_at = 9 * C * COUT
    spatial_w = weights_bf[:split_at].reshape(3, 3, C, COUT)
    temporal_w = weights_bf[split_at:].reshape(LAYERS, 3, C, C)
    frame_total = clip_pixels.shape[0]
    row_count = clip_pixels.shape[1]
    hidden = clip_pixels.reshape(frame_total // CLEN, CLEN, row_count * W, C)
    preacts = []
    columns = []
    for layer_index in range(LAYERS):
        spread = 2**layer_index
        cols = temporal_columns(hidden, spread)
        columns.append(cols)
        preact = matmul(cols, temporal_w[layer_index].reshape(3 * C, C)).reshape(hidden.shape)
        preacts.append(preact)
        hidden = (hidden.astype(jnp.float32) + jax.nn.silu(preact)).astype(jnp.bfloat16)
    cot_rows = extended_2(cotangent, (("pix", 1),), 1).reshape(frame_total, row_count + 2, W, COUT)
    row_hidden = hidden.reshape(frame_total, row_count, W * C)
    extended = extended_2(row_hidden, (("pix", 1),), 2).reshape(frame_total, row_count + 4, W, C)
    framed = jnp.pad(extended, ((0, 0), (0, 0), (1, 1), (0, 0)))
    spatial_cols = jnp.concatenate(
        [framed[:, ky : ky + row_count + 2, kx : kx + W] for ky in range(3) for kx in range(3)],
        axis=-1,
    )
    output = matmul(spatial_cols.reshape(-1, 9 * C), spatial_w.reshape(9 * C, COUT)).reshape(
        cot_rows.shape
    )
    grad_rows = (cot_rows.astype(jnp.float32) * silu_slope(output)).astype(jnp.bfloat16)
    grad_spatial = lax.dot_general(
        spatial_cols[:, 1 : row_count + 1].reshape(-1, 9 * C),
        grad_rows[:, 1 : row_count + 1].reshape(-1, COUT),
        (((0,), (0,)), ((), ())),
        preferred_element_type=jnp.float32,
    )
    row_back = conv(
        grad_rows, spatial_w[::-1, ::-1], ("NHWC", "HWOI", "NHWC"), ((0, 0), (1, 1))
    ).astype(jnp.bfloat16)
    carried_grad = row_back.reshape(frame_total // CLEN, CLEN, row_count * W, C).astype(jnp.float32)
    layer_grads = [None] * LAYERS
    for layer_index in reversed(range(LAYERS)):
        spread = 2**layer_index
        preact = preacts[layer_index]
        slope_grad_t = (carried_grad * silu_slope(preact)).astype(jnp.bfloat16)
        layer_grads[layer_index] = lax.dot_general(
            columns[layer_index],
            slope_grad_t.reshape(-1, C),
            (((0,), (0,)), ((), ())),
            preferred_element_type=jnp.float32,
        )
        if layer_index > 0:
            back_w = jnp.swapaxes(temporal_w[layer_index], 1, 2).reshape(3 * C, C)
            carried_grad = carried_grad + matmul(
                temporal_columns(slope_grad_t, spread, flip=True), back_w
            ).reshape(carried_grad.shape)
    temporal_local = jnp.stack(layer_grads).reshape(-1)
    grad_local = jnp.concatenate([grad_spatial.reshape(-1), temporal_local])
    share = grad_local.shape[0] // count
    groups = bit_groups(count) if power_of_two(count) else []
    top_low, top_width = groups[-1] if groups else (0, 0)
    top_size = 1 << top_width
    top_first = (top_size - 1) << top_low
    if groups and top_low == 2 and len(groups) == 2 and split_at >= top_first * share:
        spatial_padded = jnp.concatenate(
            [grad_spatial.reshape(-1), jnp.zeros_like(temporal_local)]
        )
        spatial_share = tree_sum_scatter(spatial_padded, "pix")
        me = lax.axis_index("pix")
        high = (me >> top_low) & (top_size - 1)
        low_mask = (1 << top_low) - 1
        top_blocks = jnp.concatenate(
            [jnp.zeros((split_at - top_first * share,), jnp.float32), temporal_local]
        ).reshape(top_size, share)
        total = top_blocks
        for offset in range(1, top_size):
            pairs = [
                (j, j ^ (offset << top_low))
                for j in range(count)
                if ((j >> top_low) & (top_size - 1)) == (top_size - 1) ^ offset
            ]
            total = total + lax.ppermute(top_blocks, "pix", pairs)
        mine = me & low_mask
        own = lax.dynamic_index_in_dim(total, mine, axis=0, keepdims=False)
        for offset in range(1, top_size):
            pairs = [
                (j, j ^ offset)
                for j in range(count)
                if ((j >> top_low) & (top_size - 1)) == top_size - 1
            ]
            send = lax.dynamic_index_in_dim(total, mine ^ offset, axis=0, keepdims=False)
            own = own + lax.ppermute(send, "pix", pairs)
        grad_share = spatial_share + jnp.where(high == top_size - 1, own, jnp.zeros_like(own))
    elif groups:
        grad_share = tree_sum_scatter(grad_local, "pix")
    else:
        grad_share = lax.psum_scatter(grad_local, "pix", scatter_dimension=0, tiled=True)
    moment_one = 0.9 * first_moment + 0.1 * grad_share
    moment_two = 0.95 * second_moment + 0.05 * grad_share * grad_share
    adam_step = moment_one / (jnp.sqrt(moment_two) + 1e-08)
    updated = (master_weights - 0.001 * adam_step).astype(jnp.bfloat16)
    if power_of_two(count):
        new_weights = tree_gather(updated, "pix")
    else:
        new_weights = lax.all_gather(updated, "pix", axis=0, tiled=True)
    return (adam_step, new_weights)


def solution(mesh):
    in_specs = (
        P("parts", "pix", None),
        P("parts", "pix", None),
        P(("parts", "pix")),
        P(("parts", "pix")),
        P(("parts", "pix")),
    )
    out_specs = (P(("parts", "pix")), P("parts"))
    return jax.shard_map(local, mesh=mesh, in_specs=in_specs, out_specs=out_specs, check_vma=False)
```

```python
import jax
import jax.numpy as jnp
from jax import lax
from jax.sharding import PartitionSpec as P

C = 64
COUT = 256
LAYERS = 3
CLEN = 32
W = 16


def extended_2(cells, sides, width):
    for axis, dim in sides:
        count = lax.axis_size(axis)
        ends = count - 1
        head = lax.slice_in_dim(cells, 0, width, axis=dim)
        tail = lax.slice_in_dim(cells, cells.shape[dim] - width, cells.shape[dim], axis=dim)
        piece = head.shape
        flat = (piece[0], -1)
        cells = jnp.concatenate(
            [
                lax.ppermute(
                    tail.reshape(flat), axis, [(i, (i + 1) % count) for i in range(ends)]
                ).reshape(piece),
                cells,
                lax.ppermute(
                    head.reshape(flat), axis, [((i + 1) % count, i) for i in range(ends)]
                ).reshape(piece),
            ],
            axis=dim,
        )
    return cells


def bit_groups(count):
    bits = count.bit_length() - 1
    return [(low, min(2, bits - low)) for low in range(0, bits, 2)]


def partners(count, low, offset):
    return [(j, j ^ (offset << low)) for j in range(count)]


def tree_sum_scatter(values, axis):
    count = lax.axis_size(axis)
    me = lax.axis_index(axis)
    blocks = values.reshape(count, -1)
    for low, width in bit_groups(count):
        size = 1 << width
        mine = (me >> low) & (size - 1)
        parts = blocks.reshape(blocks.shape[0] // size, size, blocks.shape[1])
        total = lax.dynamic_index_in_dim(parts, mine, axis=1, keepdims=False)
        for offset in range(1, size):
            send = lax.dynamic_index_in_dim(parts, mine ^ offset, axis=1, keepdims=False)
            total = total + lax.ppermute(send, axis, partners(count, low, offset))
        blocks = total
    return blocks.reshape(-1)


def tree_gather(values, axis):
    count = lax.axis_size(axis)
    me = lax.axis_index(axis)
    blocks = values.reshape(1, -1)
    for low, width in reversed(bit_groups(count)):
        size = 1 << width
        mine = (me >> low) & (size - 1)
        got = [blocks] + [
            lax.ppermute(blocks, axis, partners(count, low, offset)) for offset in range(1, size)
        ]
        stacked = jnp.stack(got)
        blocks = jnp.stack(
            [lax.dynamic_index_in_dim(stacked, part ^ mine, axis=0, keepdims=False) for part in range(size)],
            axis=1,
        ).reshape(-1, blocks.shape[1])
    return blocks.reshape(-1)


def power_of_two(count):
    return count & (count - 1) == 0


def silu_slope(value):
    sigma = jax.nn.sigmoid(value)
    return sigma * (1.0 + value * (1.0 - sigma))


def conv(lhs, rhs, dims, padding, strides=(1, 1), rhs_dilation=(1, 1)):
    return lax.conv_general_dilated(
        lhs,
        rhs,
        window_strides=strides,
        padding=padding,
        rhs_dilation=rhs_dilation,
        dimension_numbers=dims,
        preferred_element_type=jnp.float32,
    )


def temporal_columns(values, spread, flip=False):
    length = values.shape[1]
    padded = jnp.pad(values, ((0, 0), (spread, spread), (0, 0), (0, 0)))
    order = (2, 1, 0) if flip else (0, 1, 2)
    cols = jnp.concatenate(
        [padded[:, tap * spread : tap * spread + length] for tap in order], axis=-1
    )
    return cols.reshape(-1, cols.shape[-1])


def matmul(lhs, rhs):
    return jnp.dot(lhs, rhs, preferred_element_type=jnp.float32)


def local(clip_pixels, cotangent, master_weights, first_moment, second_moment):
    count = lax.axis_size("pix")
    if power_of_two(count):
        weights_bf = tree_gather(master_weights.astype(jnp.bfloat16), "pix")
    else:
        weights_bf = lax.all_gather(master_weights.astype(jnp.bfloat16), "pix", axis=0, tiled=True)
    split_at = 9 * C * COUT
    spatial_w = weights_bf[:split_at].reshape(3, 3, C, COUT)
    temporal_w = weights_bf[split_at:].reshape(LAYERS, 3, C, C)
    frame_total = clip_pixels.shape[0]
    row_count = clip_pixels.shape[1]
    hidden = clip_pixels.reshape(frame_total // CLEN, CLEN, row_count * W, C)
    preacts = []
    columns = []
    for layer_index in range(LAYERS):
        spread = 2**layer_index
        cols = temporal_columns(hidden, spread)
        columns.append(cols)
        preact = matmul(cols, temporal_w[layer_index].reshape(3 * C, C)).reshape(hidden.shape)
        preacts.append(preact)
        hidden = (hidden.astype(jnp.float32) + jax.nn.silu(preact)).astype(jnp.bfloat16)
    cot_rows = extended_2(cotangent, (("pix", 1),), 1).reshape(frame_total, row_count + 2, W, COUT)
    row_hidden = hidden.reshape(frame_total, row_count, W * C)
    extended = extended_2(row_hidden, (("pix", 1),), 2).reshape(frame_total, row_count + 4, W, C)
    framed = jnp.pad(extended, ((0, 0), (0, 0), (1, 1), (0, 0)))
    spatial_cols = jnp.concatenate(
        [framed[:, ky : ky + row_count + 2, kx : kx + W] for ky in range(3) for kx in range(3)],
        axis=-1,
    )
    output = matmul(spatial_cols.reshape(-1, 9 * C), spatial_w.reshape(9 * C, COUT)).reshape(
        cot_rows.shape
    )
    grad_rows = (cot_rows.astype(jnp.float32) * silu_slope(output)).astype(jnp.bfloat16)
    grad_spatial = lax.dot_general(
        spatial_cols[:, 1 : row_count + 1].reshape(-1, 9 * C),
        grad_rows[:, 1 : row_count + 1].reshape(-1, COUT),
        (((0,), (0,)), ((), ())),
        preferred_element_type=jnp.float32,
    )
    row_back = conv(
        grad_rows, spatial_w[::-1, ::-1], ("NHWC", "HWOI", "NHWC"), ((0, 0), (1, 1))
    ).astype(jnp.bfloat16)
    carried_grad = row_back.reshape(frame_total // CLEN, CLEN, row_count * W, C).astype(jnp.float32)
    layer_grads = [None] * LAYERS
    for layer_index in reversed(range(LAYERS)):
        spread = 2**layer_index
        preact = preacts[layer_index]
        slope_grad_t = (carried_grad * silu_slope(preact)).astype(jnp.bfloat16)
        layer_grads[layer_index] = lax.dot_general(
            columns[layer_index],
            slope_grad_t.reshape(-1, C),
            (((0,), (0,)), ((), ())),
            preferred_element_type=jnp.float32,
        )
        if layer_index > 0:
            back_w = jnp.swapaxes(temporal_w[layer_index], 1, 2).reshape(3 * C, C)
            carried_grad = carried_grad + matmul(
                temporal_columns(slope_grad_t, spread, flip=True), back_w
            ).reshape(carried_grad.shape)
    grad_local = jnp.concatenate([grad_spatial.reshape(-1), jnp.stack(layer_grads).reshape(-1)])
    if power_of_two(count):
        grad_share = tree_sum_scatter(grad_local, "pix")
    else:
        grad_share = lax.psum_scatter(grad_local, "pix", scatter_dimension=0, tiled=True)
    moment_one = 0.9 * first_moment + 0.1 * grad_share
    moment_two = 0.95 * second_moment + 0.05 * grad_share * grad_share
    adam_step = moment_one / (jnp.sqrt(moment_two) + 1e-08)
    updated = (master_weights - 0.001 * adam_step).astype(jnp.bfloat16)
    if power_of_two(count):
        new_weights = tree_gather(updated, "pix")
    else:
        new_weights = lax.all_gather(updated, "pix", axis=0, tiled=True)
    return (adam_step, new_weights)


def solution(mesh):
    in_specs = (
        P("parts", "pix", None),
        P("parts", "pix", None),
        P(("parts", "pix")),
        P(("parts", "pix")),
        P(("parts", "pix")),
    )
    out_specs = (P(("parts", "pix")), P("parts"))
    return jax.shard_map(local, mesh=mesh, in_specs=in_specs, out_specs=out_specs, check_vma=False)
```

```python
import jax
import jax.numpy as jnp
from jax import lax
from jax.sharding import PartitionSpec as P

C = 64
COUT = 256
LAYERS = 3
CLEN = 32
W = 16


def extended_2(cells, sides, width):
    for axis, dim in sides:
        count = lax.axis_size(axis)
        ends = count - 1
        head = lax.slice_in_dim(cells, 0, width, axis=dim)
        tail = lax.slice_in_dim(cells, cells.shape[dim] - width, cells.shape[dim], axis=dim)
        piece = head.shape
        flat = (piece[0], -1)
        cells = jnp.concatenate(
            [
                lax.ppermute(
                    tail.reshape(flat), axis, [(i, (i + 1) % count) for i in range(ends)]
                ).reshape(piece),
                cells,
                lax.ppermute(
                    head.reshape(flat), axis, [((i + 1) % count, i) for i in range(ends)]
                ).reshape(piece),
            ],
            axis=dim,
        )
    return cells


def bit_groups(count):
    bits = count.bit_length() - 1
    return [(low, min(2, bits - low)) for low in range(0, bits, 2)]


def partners(count, low, offset):
    return [(j, j ^ (offset << low)) for j in range(count)]


def tree_sum_scatter(values, axis):
    count = lax.axis_size(axis)
    me = lax.axis_index(axis)
    blocks = values.reshape(count, -1)
    for low, width in bit_groups(count):
        size = 1 << width
        mine = (me >> low) & (size - 1)
        parts = blocks.reshape(blocks.shape[0] // size, size, blocks.shape[1])
        total = lax.dynamic_index_in_dim(parts, mine, axis=1, keepdims=False)
        for offset in range(1, size):
            send = lax.dynamic_index_in_dim(parts, mine ^ offset, axis=1, keepdims=False)
            total = total + lax.ppermute(send, axis, partners(count, low, offset))
        blocks = total
    return blocks.reshape(-1)


def tree_gather(values, axis):
    count = lax.axis_size(axis)
    me = lax.axis_index(axis)
    blocks = values.reshape(1, -1)
    for low, width in reversed(bit_groups(count)):
        size = 1 << width
        mine = (me >> low) & (size - 1)
        got = [blocks] + [
            lax.ppermute(blocks, axis, partners(count, low, offset)) for offset in range(1, size)
        ]
        stacked = jnp.stack(got)
        blocks = jnp.stack(
            [lax.dynamic_index_in_dim(stacked, part ^ mine, axis=0, keepdims=False) for part in range(size)],
            axis=1,
        ).reshape(-1, blocks.shape[1])
    return blocks.reshape(-1)


def power_of_two(count):
    return count & (count - 1) == 0


def silu_slope(value):
    sigma = jax.nn.sigmoid(value)
    return sigma * (1.0 + value * (1.0 - sigma))


def conv(lhs, rhs, dims, padding, strides=(1, 1), rhs_dilation=(1, 1)):
    return lax.conv_general_dilated(
        lhs,
        rhs,
        window_strides=strides,
        padding=padding,
        rhs_dilation=rhs_dilation,
        dimension_numbers=dims,
        preferred_element_type=jnp.float32,
    )


def temporal_columns(values, spread, flip=False):
    length = values.shape[1]
    padded = jnp.pad(values, ((0, 0), (spread, spread), (0, 0), (0, 0)))
    order = (2, 1, 0) if flip else (0, 1, 2)
    cols = jnp.concatenate(
        [padded[:, tap * spread : tap * spread + length] for tap in order], axis=-1
    )
    return cols.reshape(-1, cols.shape[-1])


def matmul(lhs, rhs):
    return jnp.dot(lhs, rhs, preferred_element_type=jnp.float32)


def local(clip_pixels, cotangent, master_weights, first_moment, second_moment):
    count = lax.axis_size("pix")
    if power_of_two(count):
        weights_bf = tree_gather(master_weights.astype(jnp.bfloat16), "pix")
    else:
        weights_bf = lax.all_gather(master_weights.astype(jnp.bfloat16), "pix", axis=0, tiled=True)
    split_at = 9 * C * COUT
    spatial_w = weights_bf[:split_at].reshape(3, 3, C, COUT)
    temporal_w = weights_bf[split_at:].reshape(LAYERS, 3, C, C)
    frame_total = clip_pixels.shape[0]
    row_count = clip_pixels.shape[1]
    hidden = clip_pixels.reshape(frame_total // CLEN, CLEN, row_count * W, C)
    preacts = []
    columns = []
    for layer_index in range(LAYERS):
        spread = 2**layer_index
        cols = lax.optimization_barrier(temporal_columns(hidden, spread))
        columns.append(cols)
        preact = matmul(cols, temporal_w[layer_index].reshape(3 * C, C)).reshape(hidden.shape)
        preacts.append(preact)
        hidden = (hidden.astype(jnp.float32) + jax.nn.silu(preact)).astype(jnp.bfloat16)
    cot_rows = extended_2(cotangent, (("pix", 1),), 1).reshape(frame_total, row_count + 2, W, COUT)
    row_hidden = hidden.reshape(frame_total, row_count, W * C)
    extended = extended_2(row_hidden, (("pix", 1),), 2).reshape(frame_total, row_count + 4, W, C)
    framed = jnp.pad(extended, ((0, 0), (0, 0), (1, 1), (0, 0)))
    spatial_cols = jnp.concatenate(
        [framed[:, ky : ky + row_count + 2, kx : kx + W] for ky in range(3) for kx in range(3)],
        axis=-1,
    )
    output = matmul(spatial_cols.reshape(-1, 9 * C), spatial_w.reshape(9 * C, COUT)).reshape(
        cot_rows.shape
    )
    grad_rows = (cot_rows.astype(jnp.float32) * silu_slope(output)).astype(jnp.bfloat16)
    grad_spatial = lax.dot_general(
        spatial_cols[:, 1 : row_count + 1].reshape(-1, 9 * C),
        grad_rows[:, 1 : row_count + 1].reshape(-1, COUT),
        (((0,), (0,)), ((), ())),
        preferred_element_type=jnp.float32,
    )
    row_back = conv(
        grad_rows, spatial_w[::-1, ::-1], ("NHWC", "HWOI", "NHWC"), ((0, 0), (1, 1))
    ).astype(jnp.bfloat16)
    carried_grad = row_back.reshape(frame_total // CLEN, CLEN, row_count * W, C).astype(jnp.float32)
    layer_grads = [None] * LAYERS
    for layer_index in reversed(range(LAYERS)):
        spread = 2**layer_index
        preact = preacts[layer_index]
        slope_grad_t = (carried_grad * silu_slope(preact)).astype(jnp.bfloat16)
        layer_grads[layer_index] = lax.dot_general(
            columns[layer_index],
            slope_grad_t.reshape(-1, C),
            (((0,), (0,)), ((), ())),
            preferred_element_type=jnp.float32,
        )
        if layer_index > 0:
            back_w = jnp.swapaxes(temporal_w[layer_index], 1, 2).reshape(3 * C, C)
            carried_grad = carried_grad + matmul(
                temporal_columns(slope_grad_t, spread, flip=True), back_w
            ).reshape(carried_grad.shape)
    grad_local = jnp.concatenate([grad_spatial.reshape(-1), jnp.stack(layer_grads).reshape(-1)])
    if power_of_two(count):
        grad_share = tree_sum_scatter(grad_local, "pix")
    else:
        grad_share = lax.psum_scatter(grad_local, "pix", scatter_dimension=0, tiled=True)
    moment_one = 0.9 * first_moment + 0.1 * grad_share
    moment_two = 0.95 * second_moment + 0.05 * grad_share * grad_share
    adam_step = moment_one / (jnp.sqrt(moment_two) + 1e-08)
    updated = (master_weights - 0.001 * adam_step).astype(jnp.bfloat16)
    if power_of_two(count):
        new_weights = tree_gather(updated, "pix")
    else:
        new_weights = lax.all_gather(updated, "pix", axis=0, tiled=True)
    return (adam_step, new_weights)


def solution(mesh):
    in_specs = (
        P("parts", "pix", None),
        P("parts", "pix", None),
        P(("parts", "pix")),
        P(("parts", "pix")),
        P(("parts", "pix")),
    )
    out_specs = (P(("parts", "pix")), P("parts"))
    return jax.shard_map(local, mesh=mesh, in_specs=in_specs, out_specs=out_specs, check_vma=False)
```

```python
import jax
import jax.numpy as jnp
from jax import lax
from jax.sharding import PartitionSpec as P

C = 64
COUT = 256
LAYERS = 3
CLEN = 32
W = 16


def extended_2(cells, sides, width):
    for axis, dim in sides:
        count = lax.axis_size(axis)
        ends = count - 1
        head = lax.slice_in_dim(cells, 0, width, axis=dim)
        tail = lax.slice_in_dim(cells, cells.shape[dim] - width, cells.shape[dim], axis=dim)
        piece = head.shape
        flat = (piece[0], -1)
        cells = jnp.concatenate(
            [
                lax.ppermute(
                    tail.reshape(flat), axis, [(i, (i + 1) % count) for i in range(ends)]
                ).reshape(piece),
                cells,
                lax.ppermute(
                    head.reshape(flat), axis, [((i + 1) % count, i) for i in range(ends)]
                ).reshape(piece),
            ],
            axis=dim,
        )
    return cells


def bit_groups(count):
    bits = count.bit_length() - 1
    return [(low, min(2, bits - low)) for low in range(0, bits, 2)]


def partners(count, low, offset):
    return [(j, j ^ (offset << low)) for j in range(count)]


def tree_sum_scatter(values, axis):
    count = lax.axis_size(axis)
    me = lax.axis_index(axis)
    blocks = values.reshape(count, -1)
    for low, width in bit_groups(count):
        size = 1 << width
        mine = (me >> low) & (size - 1)
        parts = blocks.reshape(blocks.shape[0] // size, size, blocks.shape[1])
        total = lax.dynamic_index_in_dim(parts, mine, axis=1, keepdims=False)
        for offset in range(1, size):
            send = lax.dynamic_index_in_dim(parts, mine ^ offset, axis=1, keepdims=False)
            total = total + lax.ppermute(send, axis, partners(count, low, offset))
        blocks = total
    return blocks.reshape(-1)


def tree_gather(values, axis):
    count = lax.axis_size(axis)
    me = lax.axis_index(axis)
    blocks = values.reshape(1, -1)
    for low, width in reversed(bit_groups(count)):
        size = 1 << width
        mine = (me >> low) & (size - 1)
        got = [blocks] + [
            lax.ppermute(blocks, axis, partners(count, low, offset)) for offset in range(1, size)
        ]
        stacked = jnp.stack(got)
        blocks = jnp.stack(
            [lax.dynamic_index_in_dim(stacked, part ^ mine, axis=0, keepdims=False) for part in range(size)],
            axis=1,
        ).reshape(-1, blocks.shape[1])
    return blocks.reshape(-1)


def power_of_two(count):
    return count & (count - 1) == 0


def silu_slope(value):
    sigma = jax.nn.sigmoid(value)
    return sigma * (1.0 + value * (1.0 - sigma))


def conv(lhs, rhs, dims, padding, strides=(1, 1), rhs_dilation=(1, 1)):
    return lax.conv_general_dilated(
        lhs,
        rhs,
        window_strides=strides,
        padding=padding,
        rhs_dilation=rhs_dilation,
        dimension_numbers=dims,
        preferred_element_type=jnp.float32,
    )


def temporal_columns(values, spread, flip=False):
    length = values.shape[1]
    padded = jnp.pad(values, ((0, 0), (spread, spread), (0, 0), (0, 0)))
    order = (2, 1, 0) if flip else (0, 1, 2)
    cols = jnp.concatenate(
        [padded[:, tap * spread : tap * spread + length] for tap in order], axis=-1
    )
    return cols.reshape(-1, cols.shape[-1])


def matmul(lhs, rhs):
    return jnp.dot(lhs, rhs, preferred_element_type=jnp.float32)


def local(clip_pixels, cotangent, master_weights, first_moment, second_moment):
    count = lax.axis_size("pix")
    if power_of_two(count):
        weights_bf = tree_gather(master_weights.astype(jnp.bfloat16), "pix")
    else:
        weights_bf = lax.all_gather(master_weights.astype(jnp.bfloat16), "pix", axis=0, tiled=True)
    split_at = 9 * C * COUT
    spatial_w = weights_bf[:split_at].reshape(3, 3, C, COUT)
    temporal_w = weights_bf[split_at:].reshape(LAYERS, 3, C, C)
    frame_total = clip_pixels.shape[0]
    row_count = clip_pixels.shape[1]
    hidden = clip_pixels.reshape(frame_total // CLEN, CLEN, row_count * W, C)
    preacts = []
    columns = []
    for layer_index in range(LAYERS):
        spread = 2**layer_index
        cols = lax.optimization_barrier(temporal_columns(hidden, spread))
        columns.append(cols)
        preact = matmul(cols, temporal_w[layer_index].reshape(3 * C, C)).reshape(hidden.shape)
        preacts.append(preact)
        hidden = (hidden.astype(jnp.float32) + jax.nn.silu(preact)).astype(jnp.bfloat16)
    cot_view = lax.optimization_barrier(cotangent.reshape(frame_total, row_count, W, COUT))
    cot_rows = extended_2(cot_view.reshape(cotangent.shape), (("pix", 1),), 1).reshape(
        frame_total, row_count + 2, W, COUT
    )
    row_hidden = hidden.reshape(frame_total, row_count, W * C)
    extended = extended_2(row_hidden, (("pix", 1),), 2).reshape(frame_total, row_count + 4, W, C)
    framed = jnp.pad(extended, ((0, 0), (0, 0), (1, 1), (0, 0)))
    spatial_cols = jnp.concatenate(
        [framed[:, ky : ky + row_count + 2, kx : kx + W] for ky in range(3) for kx in range(3)],
        axis=-1,
    )
    output = matmul(spatial_cols.reshape(-1, 9 * C), spatial_w.reshape(9 * C, COUT)).reshape(
        cot_rows.shape
    )
    grad_rows = (cot_rows.astype(jnp.float32) * silu_slope(output)).astype(jnp.bfloat16)
    grad_spatial = lax.dot_general(
        spatial_cols[:, 1 : row_count + 1].reshape(-1, 9 * C),
        grad_rows[:, 1 : row_count + 1].reshape(-1, COUT),
        (((0,), (0,)), ((), ())),
        preferred_element_type=jnp.float32,
    )
    row_back = conv(
        grad_rows, spatial_w[::-1, ::-1], ("NHWC", "HWOI", "NHWC"), ((0, 0), (1, 1))
    ).astype(jnp.bfloat16)
    carried_grad = row_back.reshape(frame_total // CLEN, CLEN, row_count * W, C).astype(jnp.float32)
    layer_grads = [None] * LAYERS
    for layer_index in reversed(range(LAYERS)):
        spread = 2**layer_index
        preact = preacts[layer_index]
        slope_grad_t = (carried_grad * silu_slope(preact)).astype(jnp.bfloat16)
        layer_grads[layer_index] = lax.dot_general(
            columns[layer_index],
            slope_grad_t.reshape(-1, C),
            (((0,), (0,)), ((), ())),
            preferred_element_type=jnp.float32,
        )
        if layer_index > 0:
            back_w = jnp.swapaxes(temporal_w[layer_index], 1, 2).reshape(3 * C, C)
            carried_grad = carried_grad + matmul(
                temporal_columns(slope_grad_t, spread, flip=True), back_w
            ).reshape(carried_grad.shape)
    grad_local = jnp.concatenate([grad_spatial.reshape(-1), jnp.stack(layer_grads).reshape(-1)])
    if power_of_two(count):
        grad_share = tree_sum_scatter(grad_local, "pix")
    else:
        grad_share = lax.psum_scatter(grad_local, "pix", scatter_dimension=0, tiled=True)
    moment_one = 0.9 * first_moment + 0.1 * grad_share
    moment_two = 0.95 * second_moment + 0.05 * grad_share * grad_share
    adam_step = moment_one / (jnp.sqrt(moment_two) + 1e-08)
    updated = (master_weights - 0.001 * adam_step).astype(jnp.bfloat16)
    if power_of_two(count):
        new_weights = tree_gather(updated, "pix")
    else:
        new_weights = lax.all_gather(updated, "pix", axis=0, tiled=True)
    return (adam_step, new_weights)


def solution(mesh):
    in_specs = (
        P("parts", "pix", None),
        P("parts", "pix", None),
        P(("parts", "pix")),
        P(("parts", "pix")),
        P(("parts", "pix")),
    )
    out_specs = (P(("parts", "pix")), P("parts"))
    return jax.shard_map(local, mesh=mesh, in_specs=in_specs, out_specs=out_specs, check_vma=False)
```

```python
import jax
import jax.numpy as jnp
from jax import lax
from jax.sharding import PartitionSpec as P

C = 64
COUT = 256
LAYERS = 3
CLEN = 32
W = 16


def extended_2(cells, sides, width):
    for axis, dim in sides:
        count = lax.axis_size(axis)
        ends = count - 1
        head = lax.slice_in_dim(cells, 0, width, axis=dim)
        tail = lax.slice_in_dim(cells, cells.shape[dim] - width, cells.shape[dim], axis=dim)
        piece = head.shape
        flat = (piece[0], -1)
        cells = jnp.concatenate(
            [
                lax.ppermute(
                    tail.reshape(flat), axis, [(i, (i + 1) % count) for i in range(ends)]
                ).reshape(piece),
                cells,
                lax.ppermute(
                    head.reshape(flat), axis, [((i + 1) % count, i) for i in range(ends)]
                ).reshape(piece),
            ],
            axis=dim,
        )
    return cells


def bit_groups(count):
    bits = count.bit_length() - 1
    return [(low, min(2, bits - low)) for low in range(0, bits, 2)]


def partners(count, low, offset):
    return [(j, j ^ (offset << low)) for j in range(count)]


def tree_sum_scatter(values, axis):
    count = lax.axis_size(axis)
    me = lax.axis_index(axis)
    blocks = values.reshape(count, -1)
    for low, width in bit_groups(count):
        size = 1 << width
        mine = (me >> low) & (size - 1)
        parts = blocks.reshape(blocks.shape[0] // size, size, blocks.shape[1])
        total = lax.dynamic_index_in_dim(parts, mine, axis=1, keepdims=False)
        for offset in range(1, size):
            send = lax.dynamic_index_in_dim(parts, mine ^ offset, axis=1, keepdims=False)
            total = total + lax.ppermute(send, axis, partners(count, low, offset))
        blocks = total
    return blocks.reshape(-1)


def tree_gather(values, axis):
    count = lax.axis_size(axis)
    me = lax.axis_index(axis)
    blocks = values.reshape(1, -1)
    for low, width in reversed(bit_groups(count)):
        size = 1 << width
        mine = (me >> low) & (size - 1)
        got = [blocks] + [
            lax.ppermute(blocks, axis, partners(count, low, offset)) for offset in range(1, size)
        ]
        stacked = jnp.stack(got)
        blocks = jnp.stack(
            [lax.dynamic_index_in_dim(stacked, part ^ mine, axis=0, keepdims=False) for part in range(size)],
            axis=1,
        ).reshape(-1, blocks.shape[1])
    return blocks.reshape(-1)


def power_of_two(count):
    return count & (count - 1) == 0


def silu_slope(value):
    sigma = jax.nn.sigmoid(value)
    return sigma * (1.0 + value * (1.0 - sigma))


def conv(lhs, rhs, dims, padding, strides=(1, 1), rhs_dilation=(1, 1)):
    return lax.conv_general_dilated(
        lhs,
        rhs,
        window_strides=strides,
        padding=padding,
        rhs_dilation=rhs_dilation,
        dimension_numbers=dims,
        preferred_element_type=jnp.float32,
    )


def temporal_columns(values, spread, flip=False):
    length = values.shape[1]
    padded = jnp.pad(values, ((0, 0), (spread, spread), (0, 0), (0, 0)))
    order = (2, 1, 0) if flip else (0, 1, 2)
    cols = jnp.concatenate(
        [padded[:, tap * spread : tap * spread + length] for tap in order], axis=-1
    )
    return cols.reshape(-1, cols.shape[-1])


def matmul(lhs, rhs):
    return jnp.dot(lhs, rhs, preferred_element_type=jnp.float32)


def local(clip_pixels, cotangent, master_weights, first_moment, second_moment):
    count = lax.axis_size("pix")
    if power_of_two(count):
        weights_bf = tree_gather(master_weights.astype(jnp.bfloat16), "pix")
    else:
        weights_bf = lax.all_gather(master_weights.astype(jnp.bfloat16), "pix", axis=0, tiled=True)
    split_at = 9 * C * COUT
    spatial_w = weights_bf[:split_at].reshape(3, 3, C, COUT)
    temporal_w = weights_bf[split_at:].reshape(LAYERS, 3, C, C)
    frame_total = clip_pixels.shape[0]
    row_count = clip_pixels.shape[1]
    hidden = clip_pixels.reshape(frame_total // CLEN, CLEN, row_count * W, C)
    preacts = []
    columns = []
    for layer_index in range(LAYERS):
        spread = 2**layer_index
        cols = lax.optimization_barrier(temporal_columns(hidden, spread))
        columns.append(cols)
        preact = matmul(cols, temporal_w[layer_index].reshape(3 * C, C)).reshape(hidden.shape)
        preacts.append(preact)
        hidden = (hidden.astype(jnp.float32) + jax.nn.silu(preact)).astype(jnp.bfloat16)
    cot_view = lax.optimization_barrier(cotangent.reshape(frame_total, row_count, W, COUT))
    cot_rows = extended_2(cot_view, (("pix", 1),), 1)
    row_hidden = hidden.reshape(frame_total, row_count, W * C)
    extended = extended_2(row_hidden, (("pix", 1),), 2).reshape(frame_total, row_count + 4, W, C)
    framed = jnp.pad(extended, ((0, 0), (0, 0), (1, 1), (0, 0)))
    spatial_cols = jnp.concatenate(
        [framed[:, ky : ky + row_count + 2, kx : kx + W] for ky in range(3) for kx in range(3)],
        axis=-1,
    )
    output = matmul(spatial_cols.reshape(-1, 9 * C), spatial_w.reshape(9 * C, COUT)).reshape(
        cot_rows.shape
    )
    grad_rows = (cot_rows.astype(jnp.float32) * silu_slope(output)).astype(jnp.bfloat16)
    grad_spatial = lax.dot_general(
        spatial_cols[:, 1 : row_count + 1].reshape(-1, 9 * C),
        grad_rows[:, 1 : row_count + 1].reshape(-1, COUT),
        (((0,), (0,)), ((), ())),
        preferred_element_type=jnp.float32,
    )
    row_back = conv(
        grad_rows, spatial_w[::-1, ::-1], ("NHWC", "HWOI", "NHWC"), ((0, 0), (1, 1))
    ).astype(jnp.bfloat16)
    carried_grad = row_back.reshape(frame_total // CLEN, CLEN, row_count * W, C).astype(jnp.float32)
    layer_grads = [None] * LAYERS
    for layer_index in reversed(range(LAYERS)):
        spread = 2**layer_index
        preact = preacts[layer_index]
        slope_grad_t = (carried_grad * silu_slope(preact)).astype(jnp.bfloat16)
        layer_grads[layer_index] = lax.dot_general(
            columns[layer_index],
            slope_grad_t.reshape(-1, C),
            (((0,), (0,)), ((), ())),
            preferred_element_type=jnp.float32,
        )
        if layer_index > 0:
            back_w = jnp.swapaxes(temporal_w[layer_index], 1, 2).reshape(3 * C, C)
            carried_grad = carried_grad + matmul(
                temporal_columns(slope_grad_t, spread, flip=True), back_w
            ).reshape(carried_grad.shape)
    grad_local = jnp.concatenate([grad_spatial.reshape(-1), jnp.stack(layer_grads).reshape(-1)])
    if power_of_two(count):
        grad_share = tree_sum_scatter(grad_local, "pix")
    else:
        grad_share = lax.psum_scatter(grad_local, "pix", scatter_dimension=0, tiled=True)
    moment_one = 0.9 * first_moment + 0.1 * grad_share
    moment_two = 0.95 * second_moment + 0.05 * grad_share * grad_share
    adam_step = moment_one / (jnp.sqrt(moment_two) + 1e-08)
    updated = (master_weights - 0.001 * adam_step).astype(jnp.bfloat16)
    if power_of_two(count):
        new_weights = tree_gather(updated, "pix")
    else:
        new_weights = lax.all_gather(updated, "pix", axis=0, tiled=True)
    return (adam_step, new_weights)


def solution(mesh):
    in_specs = (
        P("parts", "pix", None),
        P("parts", "pix", None),
        P(("parts", "pix")),
        P(("parts", "pix")),
        P(("parts", "pix")),
    )
    out_specs = (P(("parts", "pix")), P("parts"))
    return jax.shard_map(local, mesh=mesh, in_specs=in_specs, out_specs=out_specs, check_vma=False)
```

```python
import jax
import jax.numpy as jnp
from jax import lax
from jax.sharding import PartitionSpec as P

C = 64
COUT = 256
LAYERS = 3
CLEN = 32
W = 16


def extended_2(cells, sides, width):
    for axis, dim in sides:
        count = lax.axis_size(axis)
        ends = count - 1
        head = lax.slice_in_dim(cells, 0, width, axis=dim)
        tail = lax.slice_in_dim(cells, cells.shape[dim] - width, cells.shape[dim], axis=dim)
        piece = head.shape
        flat = (piece[0], -1)
        cells = jnp.concatenate(
            [
                lax.ppermute(
                    tail.reshape(flat), axis, [(i, (i + 1) % count) for i in range(ends)]
                ).reshape(piece),
                cells,
                lax.ppermute(
                    head.reshape(flat), axis, [((i + 1) % count, i) for i in range(ends)]
                ).reshape(piece),
            ],
            axis=dim,
        )
    return cells


def bit_groups(count):
    bits = count.bit_length() - 1
    return [(low, min(2, bits - low)) for low in range(0, bits, 2)]


def partners(count, low, offset):
    return [(j, j ^ (offset << low)) for j in range(count)]


def tree_sum_scatter(values, axis):
    count = lax.axis_size(axis)
    me = lax.axis_index(axis)
    blocks = values.reshape(count, -1)
    for low, width in bit_groups(count):
        size = 1 << width
        mine = (me >> low) & (size - 1)
        parts = blocks.reshape(blocks.shape[0] // size, size, blocks.shape[1])
        total = lax.dynamic_index_in_dim(parts, mine, axis=1, keepdims=False)
        for offset in range(1, size):
            send = lax.dynamic_index_in_dim(parts, mine ^ offset, axis=1, keepdims=False)
            total = total + lax.ppermute(send, axis, partners(count, low, offset))
        blocks = total
    return blocks.reshape(-1)


def tree_gather(values, axis):
    count = lax.axis_size(axis)
    me = lax.axis_index(axis)
    blocks = values.reshape(1, -1)
    for low, width in reversed(bit_groups(count)):
        size = 1 << width
        mine = (me >> low) & (size - 1)
        got = [blocks] + [
            lax.ppermute(blocks, axis, partners(count, low, offset)) for offset in range(1, size)
        ]
        stacked = jnp.stack(got)
        blocks = jnp.stack(
            [lax.dynamic_index_in_dim(stacked, part ^ mine, axis=0, keepdims=False) for part in range(size)],
            axis=1,
        ).reshape(-1, blocks.shape[1])
    return blocks.reshape(-1)


def power_of_two(count):
    return count & (count - 1) == 0


def silu_slope(value):
    sigma = jax.nn.sigmoid(value)
    return sigma * (1.0 + value * (1.0 - sigma))


def conv(lhs, rhs, dims, padding, strides=(1, 1), rhs_dilation=(1, 1)):
    return lax.conv_general_dilated(
        lhs,
        rhs,
        window_strides=strides,
        padding=padding,
        rhs_dilation=rhs_dilation,
        dimension_numbers=dims,
        preferred_element_type=jnp.float32,
    )


def temporal_columns(values, spread, flip=False):
    length = values.shape[1]
    padded = jnp.pad(values, ((0, 0), (spread, spread), (0, 0), (0, 0)))
    order = (2, 1, 0) if flip else (0, 1, 2)
    cols = jnp.concatenate(
        [padded[:, tap * spread : tap * spread + length] for tap in order], axis=-1
    )
    return cols.reshape(-1, cols.shape[-1])


def matmul(lhs, rhs):
    return jnp.dot(lhs, rhs, preferred_element_type=jnp.float32)


def local(clip_pixels, cotangent, master_weights, first_moment, second_moment):
    count = lax.axis_size("pix")
    if power_of_two(count):
        weights_bf = tree_gather(master_weights.astype(jnp.bfloat16), "pix")
    else:
        weights_bf = lax.all_gather(master_weights.astype(jnp.bfloat16), "pix", axis=0, tiled=True)
    split_at = 9 * C * COUT
    spatial_w = weights_bf[:split_at].reshape(3, 3, C, COUT)
    temporal_w = weights_bf[split_at:].reshape(LAYERS, 3, C, C)
    frame_total = clip_pixels.shape[0]
    row_count = clip_pixels.shape[1]
    hidden = clip_pixels.reshape(frame_total // CLEN, CLEN, row_count * W, C)
    preacts = []
    columns = []
    for layer_index in range(LAYERS):
        spread = 2**layer_index
        cols = lax.optimization_barrier(temporal_columns(hidden, spread))
        columns.append(cols)
        preact = matmul(cols, temporal_w[layer_index].reshape(3 * C, C)).reshape(hidden.shape)
        preacts.append(preact)
        hidden = (hidden.astype(jnp.float32) + jax.nn.silu(preact)).astype(jnp.bfloat16)
    cot_view = lax.optimization_barrier(cotangent.reshape(frame_total, row_count, W, COUT))
    cot_rows = extended_2(cot_view, (("pix", 1),), 1)
    row_hidden = hidden.reshape(frame_total, row_count, W * C)
    extended = extended_2(row_hidden, (("pix", 1),), 2).reshape(frame_total, row_count + 4, W, C)
    framed = jnp.pad(extended, ((0, 0), (0, 0), (1, 1), (0, 0)))
    spatial_cols = jnp.concatenate(
        [framed[:, ky : ky + row_count + 2, kx : kx + W] for ky in range(3) for kx in range(3)],
        axis=-1,
    )
    output = matmul(spatial_cols.reshape(-1, 9 * C), spatial_w.reshape(9 * C, COUT)).reshape(
        cot_rows.shape
    )
    grad_rows = (cot_rows.astype(jnp.float32) * silu_slope(output)).astype(jnp.bfloat16)
    grad_spatial = lax.dot_general(
        spatial_cols[:, 1 : row_count + 1].reshape(-1, 9 * C),
        grad_rows[:, 1 : row_count + 1].reshape(-1, COUT),
        (((0,), (0,)), ((), ())),
        preferred_element_type=jnp.float32,
    )
    row_back = conv(
        grad_rows, spatial_w[::-1, ::-1], ("NHWC", "HWOI", "NHWC"), ((0, 0), (1, 1))
    ).astype(jnp.bfloat16)
    row_back = lax.optimization_barrier(row_back)
    carried_grad = row_back.reshape(frame_total // CLEN, CLEN, row_count * W, C).astype(jnp.float32)
    layer_grads = [None] * LAYERS
    for layer_index in reversed(range(LAYERS)):
        spread = 2**layer_index
        preact = preacts[layer_index]
        slope_grad_t = (carried_grad * silu_slope(preact)).astype(jnp.bfloat16)
        layer_grads[layer_index] = lax.dot_general(
            columns[layer_index],
            slope_grad_t.reshape(-1, C),
            (((0,), (0,)), ((), ())),
            preferred_element_type=jnp.float32,
        )
        if layer_index > 0:
            back_w = jnp.swapaxes(temporal_w[layer_index], 1, 2).reshape(3 * C, C)
            carried_grad = carried_grad + matmul(
                temporal_columns(slope_grad_t, spread, flip=True), back_w
            ).reshape(carried_grad.shape)
    grad_local = jnp.concatenate([grad_spatial.reshape(-1), jnp.stack(layer_grads).reshape(-1)])
    if power_of_two(count):
        grad_share = tree_sum_scatter(grad_local, "pix")
    else:
        grad_share = lax.psum_scatter(grad_local, "pix", scatter_dimension=0, tiled=True)
    moment_one = 0.9 * first_moment + 0.1 * grad_share
    moment_two = 0.95 * second_moment + 0.05 * grad_share * grad_share
    adam_step = moment_one / (jnp.sqrt(moment_two) + 1e-08)
    updated = (master_weights - 0.001 * adam_step).astype(jnp.bfloat16)
    if power_of_two(count):
        new_weights = tree_gather(updated, "pix")
    else:
        new_weights = lax.all_gather(updated, "pix", axis=0, tiled=True)
    return (adam_step, new_weights)


def solution(mesh):
    in_specs = (
        P("parts", "pix", None),
        P("parts", "pix", None),
        P(("parts", "pix")),
        P(("parts", "pix")),
        P(("parts", "pix")),
    )
    out_specs = (P(("parts", "pix")), P("parts"))
    return jax.shard_map(local, mesh=mesh, in_specs=in_specs, out_specs=out_specs, check_vma=False)
```

```python
import jax
import jax.numpy as jnp
from jax import lax
from jax.sharding import PartitionSpec as P

C = 64
COUT = 256
LAYERS = 3
CLEN = 32
W = 16


def extended_2(cells, sides, width):
    for axis, dim in sides:
        count = lax.axis_size(axis)
        ends = count - 1
        head = lax.slice_in_dim(cells, 0, width, axis=dim)
        tail = lax.slice_in_dim(cells, cells.shape[dim] - width, cells.shape[dim], axis=dim)
        piece = head.shape
        flat = (piece[0], -1)
        cells = jnp.concatenate(
            [
                lax.ppermute(
                    tail.reshape(flat), axis, [(i, (i + 1) % count) for i in range(ends)]
                ).reshape(piece),
                cells,
                lax.ppermute(
                    head.reshape(flat), axis, [((i + 1) % count, i) for i in range(ends)]
                ).reshape(piece),
            ],
            axis=dim,
        )
    return cells


def bit_groups(count):
    bits = count.bit_length() - 1
    return [(low, min(2, bits - low)) for low in range(0, bits, 2)]


def partners(count, low, offset):
    return [(j, j ^ (offset << low)) for j in range(count)]


def tree_sum_scatter(values, axis):
    count = lax.axis_size(axis)
    me = lax.axis_index(axis)
    blocks = values.reshape(count, -1)
    for low, width in bit_groups(count):
        size = 1 << width
        mine = (me >> low) & (size - 1)
        parts = blocks.reshape(blocks.shape[0] // size, size, blocks.shape[1])
        total = lax.dynamic_index_in_dim(parts, mine, axis=1, keepdims=False)
        for offset in range(1, size):
            send = lax.dynamic_index_in_dim(parts, mine ^ offset, axis=1, keepdims=False)
            total = total + lax.ppermute(send, axis, partners(count, low, offset))
        blocks = total
    return blocks.reshape(-1)


def tree_gather(values, axis):
    count = lax.axis_size(axis)
    me = lax.axis_index(axis)
    blocks = values.reshape(1, -1)
    for low, width in reversed(bit_groups(count)):
        size = 1 << width
        mine = (me >> low) & (size - 1)
        got = [blocks] + [
            lax.ppermute(blocks, axis, partners(count, low, offset)) for offset in range(1, size)
        ]
        stacked = jnp.stack(got)
        blocks = jnp.stack(
            [lax.dynamic_index_in_dim(stacked, part ^ mine, axis=0, keepdims=False) for part in range(size)],
            axis=1,
        ).reshape(-1, blocks.shape[1])
    return blocks.reshape(-1)


def power_of_two(count):
    return count & (count - 1) == 0


def silu_slope(value):
    sigma = jax.nn.sigmoid(value)
    return sigma * (1.0 + value * (1.0 - sigma))


def conv(lhs, rhs, dims, padding, strides=(1, 1), rhs_dilation=(1, 1)):
    return lax.conv_general_dilated(
        lhs,
        rhs,
        window_strides=strides,
        padding=padding,
        rhs_dilation=rhs_dilation,
        dimension_numbers=dims,
        preferred_element_type=jnp.float32,
    )


def temporal_columns(values, spread, flip=False):
    length = values.shape[1]
    padded = jnp.pad(values, ((0, 0), (spread, spread), (0, 0), (0, 0)))
    order = (2, 1, 0) if flip else (0, 1, 2)
    cols = jnp.concatenate(
        [padded[:, tap * spread : tap * spread + length] for tap in order], axis=-1
    )
    return cols.reshape(-1, cols.shape[-1])


def matmul(lhs, rhs):
    return jnp.dot(lhs, rhs, preferred_element_type=jnp.float32)


def local(clip_pixels, cotangent, master_weights, first_moment, second_moment):
    count = lax.axis_size("pix")
    if power_of_two(count):
        weights_bf = tree_gather(master_weights.astype(jnp.bfloat16), "pix")
    else:
        weights_bf = lax.all_gather(master_weights.astype(jnp.bfloat16), "pix", axis=0, tiled=True)
    split_at = 9 * C * COUT
    spatial_w = weights_bf[:split_at].reshape(3, 3, C, COUT)
    temporal_w = weights_bf[split_at:].reshape(LAYERS, 3, C, C)
    frame_total = clip_pixels.shape[0]
    row_count = clip_pixels.shape[1]
    hidden = lax.optimization_barrier(clip_pixels.reshape(frame_total // CLEN, CLEN, row_count * W, C))
    preacts = []
    columns = []
    for layer_index in range(LAYERS):
        spread = 2**layer_index
        cols = lax.optimization_barrier(temporal_columns(hidden, spread))
        columns.append(cols)
        preact = matmul(cols, temporal_w[layer_index].reshape(3 * C, C)).reshape(hidden.shape)
        preacts.append(preact)
        hidden = (hidden.astype(jnp.float32) + jax.nn.silu(preact)).astype(jnp.bfloat16)
    cot_view = lax.optimization_barrier(cotangent.reshape(frame_total, row_count, W, COUT))
    cot_rows = extended_2(cot_view, (("pix", 1),), 1)
    row_hidden = hidden.reshape(frame_total, row_count, W * C)
    extended = extended_2(row_hidden, (("pix", 1),), 2).reshape(frame_total, row_count + 4, W, C)
    framed = jnp.pad(extended, ((0, 0), (0, 0), (1, 1), (0, 0)))
    spatial_cols = jnp.concatenate(
        [framed[:, ky : ky + row_count + 2, kx : kx + W] for ky in range(3) for kx in range(3)],
        axis=-1,
    )
    output = matmul(spatial_cols.reshape(-1, 9 * C), spatial_w.reshape(9 * C, COUT)).reshape(
        cot_rows.shape
    )
    grad_rows = (cot_rows.astype(jnp.float32) * silu_slope(output)).astype(jnp.bfloat16)
    grad_spatial = lax.dot_general(
        spatial_cols[:, 1 : row_count + 1].reshape(-1, 9 * C),
        grad_rows[:, 1 : row_count + 1].reshape(-1, COUT),
        (((0,), (0,)), ((), ())),
        preferred_element_type=jnp.float32,
    )
    row_back = conv(
        grad_rows, spatial_w[::-1, ::-1], ("NHWC", "HWOI", "NHWC"), ((0, 0), (1, 1))
    ).astype(jnp.bfloat16)
    row_back = lax.optimization_barrier(row_back)
    carried_grad = row_back.reshape(frame_total // CLEN, CLEN, row_count * W, C).astype(jnp.float32)
    layer_grads = [None] * LAYERS
    for layer_index in reversed(range(LAYERS)):
        spread = 2**layer_index
        preact = preacts[layer_index]
        slope_grad_t = (carried_grad * silu_slope(preact)).astype(jnp.bfloat16)
        layer_grads[layer_index] = lax.dot_general(
            columns[layer_index],
            slope_grad_t.reshape(-1, C),
            (((0,), (0,)), ((), ())),
            preferred_element_type=jnp.float32,
        )
        if layer_index > 0:
            back_w = jnp.swapaxes(temporal_w[layer_index], 1, 2).reshape(3 * C, C)
            carried_grad = carried_grad + matmul(
                temporal_columns(slope_grad_t, spread, flip=True), back_w
            ).reshape(carried_grad.shape)
    grad_local = jnp.concatenate([grad_spatial.reshape(-1), jnp.stack(layer_grads).reshape(-1)])
    if power_of_two(count):
        grad_share = tree_sum_scatter(grad_local, "pix")
    else:
        grad_share = lax.psum_scatter(grad_local, "pix", scatter_dimension=0, tiled=True)
    moment_one = 0.9 * first_moment + 0.1 * grad_share
    moment_two = 0.95 * second_moment + 0.05 * grad_share * grad_share
    adam_step = moment_one / (jnp.sqrt(moment_two) + 1e-08)
    updated = (master_weights - 0.001 * adam_step).astype(jnp.bfloat16)
    if power_of_two(count):
        new_weights = tree_gather(updated, "pix")
    else:
        new_weights = lax.all_gather(updated, "pix", axis=0, tiled=True)
    return (adam_step, new_weights)


def solution(mesh):
    in_specs = (
        P("parts", "pix", None),
        P("parts", "pix", None),
        P(("parts", "pix")),
        P(("parts", "pix")),
        P(("parts", "pix")),
    )
    out_specs = (P(("parts", "pix")), P("parts"))
    return jax.shard_map(local, mesh=mesh, in_specs=in_specs, out_specs=out_specs, check_vma=False)
```

```python
import jax
import jax.numpy as jnp
from jax import lax
from jax.sharding import PartitionSpec as P

C = 64
COUT = 256
LAYERS = 3
CLEN = 32
W = 16


def extended_2(cells, sides, width):
    for axis, dim in sides:
        count = lax.axis_size(axis)
        ends = count - 1
        head = lax.slice_in_dim(cells, 0, width, axis=dim)
        tail = lax.slice_in_dim(cells, cells.shape[dim] - width, cells.shape[dim], axis=dim)
        piece = head.shape
        flat = (piece[0], -1)
        cells = jnp.concatenate(
            [
                lax.ppermute(
                    tail.reshape(flat), axis, [(i, (i + 1) % count) for i in range(ends)]
                ).reshape(piece),
                cells,
                lax.ppermute(
                    head.reshape(flat), axis, [((i + 1) % count, i) for i in range(ends)]
                ).reshape(piece),
            ],
            axis=dim,
        )
    return cells


def bit_groups(count):
    bits = count.bit_length() - 1
    return [(low, min(2, bits - low)) for low in range(0, bits, 2)]


def partners(count, low, offset):
    return [(j, j ^ (offset << low)) for j in range(count)]


def tree_sum_scatter(values, axis):
    count = lax.axis_size(axis)
    me = lax.axis_index(axis)
    blocks = values.reshape(count, -1)
    for low, width in bit_groups(count):
        size = 1 << width
        mine = (me >> low) & (size - 1)
        parts = blocks.reshape(blocks.shape[0] // size, size, blocks.shape[1])
        total = lax.dynamic_index_in_dim(parts, mine, axis=1, keepdims=False)
        for offset in range(1, size):
            send = lax.dynamic_index_in_dim(parts, mine ^ offset, axis=1, keepdims=False)
            total = total + lax.ppermute(send, axis, partners(count, low, offset))
        blocks = total
    return blocks.reshape(-1)


def tree_gather(values, axis):
    count = lax.axis_size(axis)
    me = lax.axis_index(axis)
    blocks = values.reshape(1, -1)
    for low, width in reversed(bit_groups(count)):
        size = 1 << width
        mine = (me >> low) & (size - 1)
        got = [blocks] + [
            lax.ppermute(blocks, axis, partners(count, low, offset)) for offset in range(1, size)
        ]
        stacked = jnp.stack(got)
        blocks = jnp.stack(
            [lax.dynamic_index_in_dim(stacked, part ^ mine, axis=0, keepdims=False) for part in range(size)],
            axis=1,
        ).reshape(-1, blocks.shape[1])
    return blocks.reshape(-1)


def power_of_two(count):
    return count & (count - 1) == 0


def silu_slope(value):
    sigma = jax.nn.sigmoid(value)
    return sigma * (1.0 + value * (1.0 - sigma))


def conv(lhs, rhs, dims, padding, strides=(1, 1), rhs_dilation=(1, 1)):
    return lax.conv_general_dilated(
        lhs,
        rhs,
        window_strides=strides,
        padding=padding,
        rhs_dilation=rhs_dilation,
        dimension_numbers=dims,
        preferred_element_type=jnp.float32,
    )


def temporal_columns(values, spread, flip=False):
    length = values.shape[1]
    padded = jnp.pad(values, ((0, 0), (spread, spread), (0, 0), (0, 0)))
    order = (2, 1, 0) if flip else (0, 1, 2)
    cols = jnp.concatenate(
        [padded[:, tap * spread : tap * spread + length] for tap in order], axis=-1
    )
    return cols.reshape(-1, cols.shape[-1])


def matmul(lhs, rhs):
    return jnp.dot(lhs, rhs, preferred_element_type=jnp.float32)


def local(clip_pixels, cotangent, master_weights, first_moment, second_moment):
    count = lax.axis_size("pix")
    if power_of_two(count):
        weights_bf = tree_gather(master_weights.astype(jnp.bfloat16), "pix")
    else:
        weights_bf = lax.all_gather(master_weights.astype(jnp.bfloat16), "pix", axis=0, tiled=True)
    split_at = 9 * C * COUT
    spatial_w = weights_bf[:split_at].reshape(3, 3, C, COUT)
    temporal_w = weights_bf[split_at:].reshape(LAYERS, 3, C, C)
    frame_total = clip_pixels.shape[0]
    row_count = clip_pixels.shape[1]
    hidden = lax.optimization_barrier(clip_pixels.reshape(frame_total // CLEN, CLEN, row_count * W, C))
    preacts = []
    columns = []
    for layer_index in range(LAYERS):
        spread = 2**layer_index
        cols = lax.optimization_barrier(temporal_columns(hidden, spread))
        columns.append(cols)
        preact = matmul(cols, temporal_w[layer_index].reshape(3 * C, C)).reshape(hidden.shape)
        preacts.append(preact)
        hidden = (hidden.astype(jnp.float32) + jax.nn.silu(preact)).astype(jnp.bfloat16)
    cot_view = lax.optimization_barrier(cotangent.reshape(frame_total, row_count, W, COUT))
    cot_rows = extended_2(cot_view, (("pix", 1),), 1)
    row_hidden = lax.optimization_barrier(hidden.reshape(frame_total, row_count, W * C))
    extended = extended_2(row_hidden, (("pix", 1),), 2).reshape(frame_total, row_count + 4, W, C)
    framed = jnp.pad(extended, ((0, 0), (0, 0), (1, 1), (0, 0)))
    spatial_cols = jnp.concatenate(
        [framed[:, ky : ky + row_count + 2, kx : kx + W] for ky in range(3) for kx in range(3)],
        axis=-1,
    )
    output = matmul(spatial_cols.reshape(-1, 9 * C), spatial_w.reshape(9 * C, COUT)).reshape(
        cot_rows.shape
    )
    grad_rows = (cot_rows.astype(jnp.float32) * silu_slope(output)).astype(jnp.bfloat16)
    grad_spatial = lax.dot_general(
        spatial_cols[:, 1 : row_count + 1].reshape(-1, 9 * C),
        grad_rows[:, 1 : row_count + 1].reshape(-1, COUT),
        (((0,), (0,)), ((), ())),
        preferred_element_type=jnp.float32,
    )
    row_back = conv(
        grad_rows, spatial_w[::-1, ::-1], ("NHWC", "HWOI", "NHWC"), ((0, 0), (1, 1))
    ).astype(jnp.bfloat16)
    row_back = lax.optimization_barrier(row_back)
    carried_grad = row_back.reshape(frame_total // CLEN, CLEN, row_count * W, C).astype(jnp.float32)
    layer_grads = [None] * LAYERS
    for layer_index in reversed(range(LAYERS)):
        spread = 2**layer_index
        preact = preacts[layer_index]
        slope_grad_t = (carried_grad * silu_slope(preact)).astype(jnp.bfloat16)
        layer_grads[layer_index] = lax.dot_general(
            columns[layer_index],
            slope_grad_t.reshape(-1, C),
            (((0,), (0,)), ((), ())),
            preferred_element_type=jnp.float32,
        )
        if layer_index > 0:
            back_w = jnp.swapaxes(temporal_w[layer_index], 1, 2).reshape(3 * C, C)
            carried_grad = carried_grad + matmul(
                temporal_columns(slope_grad_t, spread, flip=True), back_w
            ).reshape(carried_grad.shape)
    grad_local = jnp.concatenate([grad_spatial.reshape(-1), jnp.stack(layer_grads).reshape(-1)])
    if power_of_two(count):
        grad_share = tree_sum_scatter(grad_local, "pix")
    else:
        grad_share = lax.psum_scatter(grad_local, "pix", scatter_dimension=0, tiled=True)
    moment_one = 0.9 * first_moment + 0.1 * grad_share
    moment_two = 0.95 * second_moment + 0.05 * grad_share * grad_share
    adam_step = moment_one / (jnp.sqrt(moment_two) + 1e-08)
    updated = (master_weights - 0.001 * adam_step).astype(jnp.bfloat16)
    if power_of_two(count):
        new_weights = tree_gather(updated, "pix")
    else:
        new_weights = lax.all_gather(updated, "pix", axis=0, tiled=True)
    return (adam_step, new_weights)


def solution(mesh):
    in_specs = (
        P("parts", "pix", None),
        P("parts", "pix", None),
        P(("parts", "pix")),
        P(("parts", "pix")),
        P(("parts", "pix")),
    )
    out_specs = (P(("parts", "pix")), P("parts"))
    return jax.shard_map(local, mesh=mesh, in_specs=in_specs, out_specs=out_specs, check_vma=False)
```

```python
import jax
import jax.numpy as jnp
from jax import lax
from jax.sharding import PartitionSpec as P

C = 64
COUT = 256
LAYERS = 3
CLEN = 32
W = 16


def extended_2(cells, sides, width):
    for axis, dim in sides:
        count = lax.axis_size(axis)
        ends = count - 1
        head = lax.slice_in_dim(cells, 0, width, axis=dim)
        tail = lax.slice_in_dim(cells, cells.shape[dim] - width, cells.shape[dim], axis=dim)
        piece = head.shape
        flat = (piece[0], -1)
        cells = jnp.concatenate(
            [
                lax.ppermute(
                    tail.reshape(flat), axis, [(i, (i + 1) % count) for i in range(ends)]
                ).reshape(piece),
                cells,
                lax.ppermute(
                    head.reshape(flat), axis, [((i + 1) % count, i) for i in range(ends)]
                ).reshape(piece),
            ],
            axis=dim,
        )
    return cells


def bit_groups(count):
    bits = count.bit_length() - 1
    return [(low, 1) for low in range(bits)]


def partners(count, low, offset):
    return [(j, j ^ (offset << low)) for j in range(count)]


def tree_sum_scatter(values, axis):
    count = lax.axis_size(axis)
    me = lax.axis_index(axis)
    blocks = values.reshape(count, -1)
    for low, width in bit_groups(count):
        size = 1 << width
        mine = (me >> low) & (size - 1)
        parts = blocks.reshape(blocks.shape[0] // size, size, blocks.shape[1])
        total = lax.dynamic_index_in_dim(parts, mine, axis=1, keepdims=False)
        for offset in range(1, size):
            send = lax.dynamic_index_in_dim(parts, mine ^ offset, axis=1, keepdims=False)
            total = total + lax.ppermute(send, axis, partners(count, low, offset))
        blocks = total
    return blocks.reshape(-1)


def tree_gather(values, axis):
    count = lax.axis_size(axis)
    me = lax.axis_index(axis)
    blocks = values.reshape(1, -1)
    for low, width in reversed(bit_groups(count)):
        size = 1 << width
        mine = (me >> low) & (size - 1)
        got = [blocks] + [
            lax.ppermute(blocks, axis, partners(count, low, offset)) for offset in range(1, size)
        ]
        stacked = jnp.stack(got)
        blocks = jnp.stack(
            [lax.dynamic_index_in_dim(stacked, part ^ mine, axis=0, keepdims=False) for part in range(size)],
            axis=1,
        ).reshape(-1, blocks.shape[1])
    return blocks.reshape(-1)


def power_of_two(count):
    return count & (count - 1) == 0


def silu_slope(value):
    sigma = jax.nn.sigmoid(value)
    return sigma * (1.0 + value * (1.0 - sigma))


def conv(lhs, rhs, dims, padding, strides=(1, 1), rhs_dilation=(1, 1)):
    return lax.conv_general_dilated(
        lhs,
        rhs,
        window_strides=strides,
        padding=padding,
        rhs_dilation=rhs_dilation,
        dimension_numbers=dims,
        preferred_element_type=jnp.float32,
    )


def temporal_columns(values, spread, flip=False):
    length = values.shape[1]
    padded = jnp.pad(values, ((0, 0), (spread, spread), (0, 0), (0, 0)))
    order = (2, 1, 0) if flip else (0, 1, 2)
    cols = jnp.concatenate(
        [padded[:, tap * spread : tap * spread + length] for tap in order], axis=-1
    )
    return cols.reshape(-1, cols.shape[-1])


def matmul(lhs, rhs):
    return jnp.dot(lhs, rhs, preferred_element_type=jnp.float32)


def local(clip_pixels, cotangent, master_weights, first_moment, second_moment):
    count = lax.axis_size("pix")
    if power_of_two(count):
        weights_bf = tree_gather(master_weights.astype(jnp.bfloat16), "pix")
    else:
        weights_bf = lax.all_gather(master_weights.astype(jnp.bfloat16), "pix", axis=0, tiled=True)
    split_at = 9 * C * COUT
    spatial_w = weights_bf[:split_at].reshape(3, 3, C, COUT)
    temporal_w = weights_bf[split_at:].reshape(LAYERS, 3, C, C)
    frame_total = clip_pixels.shape[0]
    row_count = clip_pixels.shape[1]
    hidden = lax.optimization_barrier(clip_pixels.reshape(frame_total // CLEN, CLEN, row_count * W, C))
    preacts = []
    columns = []
    for layer_index in range(LAYERS):
        spread = 2**layer_index
        cols = lax.optimization_barrier(temporal_columns(hidden, spread))
        columns.append(cols)
        preact = matmul(cols, temporal_w[layer_index].reshape(3 * C, C)).reshape(hidden.shape)
        preacts.append(preact)
        hidden = (hidden.astype(jnp.float32) + jax.nn.silu(preact)).astype(jnp.bfloat16)
    cot_view = lax.optimization_barrier(cotangent.reshape(frame_total, row_count, W, COUT))
    cot_rows = extended_2(cot_view, (("pix", 1),), 1)
    row_hidden = lax.optimization_barrier(hidden.reshape(frame_total, row_count, W * C))
    extended = extended_2(row_hidden, (("pix", 1),), 2).reshape(frame_total, row_count + 4, W, C)
    framed = jnp.pad(extended, ((0, 0), (0, 0), (1, 1), (0, 0)))
    spatial_cols = jnp.concatenate(
        [framed[:, ky : ky + row_count + 2, kx : kx + W] for ky in range(3) for kx in range(3)],
        axis=-1,
    )
    output = matmul(spatial_cols.reshape(-1, 9 * C), spatial_w.reshape(9 * C, COUT)).reshape(
        cot_rows.shape
    )
    grad_rows = (cot_rows.astype(jnp.float32) * silu_slope(output)).astype(jnp.bfloat16)
    grad_spatial = lax.dot_general(
        spatial_cols[:, 1 : row_count + 1].reshape(-1, 9 * C),
        grad_rows[:, 1 : row_count + 1].reshape(-1, COUT),
        (((0,), (0,)), ((), ())),
        preferred_element_type=jnp.float32,
    )
    row_back = conv(
        grad_rows, spatial_w[::-1, ::-1], ("NHWC", "HWOI", "NHWC"), ((0, 0), (1, 1))
    ).astype(jnp.bfloat16)
    row_back = lax.optimization_barrier(row_back)
    carried_grad = row_back.reshape(frame_total // CLEN, CLEN, row_count * W, C).astype(jnp.float32)
    layer_grads = [None] * LAYERS
    for layer_index in reversed(range(LAYERS)):
        spread = 2**layer_index
        preact = preacts[layer_index]
        slope_grad_t = (carried_grad * silu_slope(preact)).astype(jnp.bfloat16)
        layer_grads[layer_index] = lax.dot_general(
            columns[layer_index],
            slope_grad_t.reshape(-1, C),
            (((0,), (0,)), ((), ())),
            preferred_element_type=jnp.float32,
        )
        if layer_index > 0:
            back_w = jnp.swapaxes(temporal_w[layer_index], 1, 2).reshape(3 * C, C)
            carried_grad = carried_grad + matmul(
                temporal_columns(slope_grad_t, spread, flip=True), back_w
            ).reshape(carried_grad.shape)
    grad_local = jnp.concatenate([grad_spatial.reshape(-1), jnp.stack(layer_grads).reshape(-1)])
    if power_of_two(count):
        grad_share = tree_sum_scatter(grad_local, "pix")
    else:
        grad_share = lax.psum_scatter(grad_local, "pix", scatter_dimension=0, tiled=True)
    moment_one = 0.9 * first_moment + 0.1 * grad_share
    moment_two = 0.95 * second_moment + 0.05 * grad_share * grad_share
    adam_step = moment_one / (jnp.sqrt(moment_two) + 1e-08)
    updated = (master_weights - 0.001 * adam_step).astype(jnp.bfloat16)
    if power_of_two(count):
        new_weights = tree_gather(updated, "pix")
    else:
        new_weights = lax.all_gather(updated, "pix", axis=0, tiled=True)
    return (adam_step, new_weights)


def solution(mesh):
    in_specs = (
        P("parts", "pix", None),
        P("parts", "pix", None),
        P(("parts", "pix")),
        P(("parts", "pix")),
        P(("parts", "pix")),
    )
    out_specs = (P(("parts", "pix")), P("parts"))
    return jax.shard_map(local, mesh=mesh, in_specs=in_specs, out_specs=out_specs, check_vma=False)
```
